128 devices in a mesh: gx: 8 (over z, core), gy: 16 (over y, x).
Axes of the slice: x: 4, y: 4, z: 4, core: 2. Of those that a mesh axis runs over, the one named last changes fastest.
Arguments:
- hidden_in: bfloat16 [32768, 3584], P(('gx', 'gy')), may hold values from -6 to 6
- lengths: int32 [8, 4], P('gx'), may hold values from 1 to 2048, 4096 in all within a row
- attn_norm: float32 [3584], replicated, may hold values from 0.5 to 1.5
- qkv_weight: bfloat16 [3584, 4608], P('gx', 'gy'), may hold values from -0.09375 to 0.09375
- qkv_bias: float32 [4608], replicated, may hold values from -5 to 5
Outputs:
- attn: bfloat16 [32768, 3584], P(('gx', 'gy'))
- kv_rows: bfloat16 [32768, 1024], P(('gx', 'gy'))
The draws below stay inside these ranges and needn't reach their ends.
Inputs may be any that keep to these rules, and one draw needn't show every extreme that they name: Each row of lengths sums to 4096; the longest of each row is exactly 2048.
All inputs are finite; a program needn't handle non-finite values.
Results may differ from the reference program's by a relative error of at most 0.0035.
The reference program's roundings to bfloat16 on the way (of `normed`, `joined`, `queries` and `weights`) count: a program that leaves them out, or rounds other values in their place, can miss the bound.
Values may be sent and summed in bfloat16 or wider, within the bound.
No kernel may reach another device: no remote copies, remote signals or barrier semaphores. Data moves between devices by JAX's collectives and lax.ppermute only.
A program may use at most 128 MiB of HBM per device.

```python
import math
import jax
import jax.numpy as jnp
import numpy as np
from jax import lax

D = 3584
HEADS = 28
KV_HEADS = 4
HEAD_DIM = 128
NSEQ = 4
QKV = 4608
TOK_GRP = 4096
TOKENS = 32768
MAXLEN = 2048
N_GX = 8


def draw_qkv_bias(key, part):
    qdim = HEADS * HEAD_DIM
    kdim = KV_HEADS * HEAD_DIM
    group = HEADS // KV_HEADS
    first_key, second_key, third_key = jax.random.split(key, 3)
    baseline = jnp.clip(0.5 * jax.random.normal(first_key, (QKV,), jnp.float32), -3.0, 3.0)
    chosen = jax.random.randint(second_key, (), 0, KV_HEADS)
    sign_pattern = jnp.where(jax.random.bernoulli(third_key, 0.5, (HEAD_DIM,)), 1.0, -1.0).astype(jnp.float32)
    columns = jnp.arange(QKV, dtype=jnp.int32)
    head_index = columns // HEAD_DIM
    within = columns % HEAD_DIM
    pattern = sign_pattern[within]
    member = (head_index % group).astype(jnp.float32)
    strength = 1.0 + 4.0 * member / max(group - 1, 1)
    is_query = (columns < qdim) & (head_index // group == chosen)
    is_key = (columns >= qdim) & (columns < qdim + kdim) & (head_index - HEADS == chosen)
    result = jnp.where(is_query, strength * pattern, jnp.where(is_key, 5.0 * pattern, baseline))
    return result.astype(jnp.float32)


def steps_of(key, dims, cuts, smallest, largest):
    level, own = 1.0, jax.random.fold_in(key, 6)
    for axis_at, blocks in cuts:
        steps = jnp.exp(jax.random.uniform(jax.random.fold_in(own, axis_at), (blocks,), jnp.float32, smallest / len(cuts), largest / len(cuts)))
        level = level * jnp.repeat(steps, dims[axis_at] // blocks).reshape([-1 if axis == axis_at else 1 for axis in range(len(dims))])
    return level


def profile(amount, total, limit, lean):
    portions = [(1 << 20) // math.isqrt(standing ** lean) + 1 for standing in range(2, amount + 1)]
    surplus, counts = total - limit - (amount - 1), [1] * (amount - 1)
    while surplus > 0:
        free = [i for i in range(amount - 1) if counts[i] < limit]
        mass, remaining = sum([portions[i] for i in free]), surplus
        for i in free:
            extra = min(limit - counts[i], max(1, remaining * portions[i] // mass), surplus)
            counts[i] = counts[i] + extra
            surplus = surplus - extra
    return np.array([limit] + counts)


def ragged_sizes(stream_key, count, total, bound, lean):
    if count == 2:
        one = jax.random.randint(stream_key, (), max(1, total - bound), min(bound, total - 1) + 1)
        return jnp.stack([one, total - one])
    sizes = jnp.asarray(profile(count, total, bound, lean), jnp.int32)
    couples = (count - 1) // 2
    donor, taker = sizes[1:1 + 2 * couples:2], sizes[2:2 + 2 * couples:2]
    margin = jnp.minimum(donor - 1, bound - taker)
    passed = jax.random.randint(jax.random.fold_in(stream_key, 1), (couples,), 0, 1 << 20) % (margin + 1)
    sizes = sizes.at[1:1 + 2 * couples:2].set(donor - passed).at[2:2 + 2 * couples:2].set(taker + passed)
    return sizes[jax.random.permutation(jax.random.fold_in(stream_key, 2), count)]


def gaussian(stream_key, extent, scale, reach, pieces=(), kind=jnp.bfloat16):
    loudness = steps_of(stream_key, extent, pieces, -0.22, 0.18) if pieces else 1.0
    values = jax.random.normal(stream_key, extent, jnp.float32) * scale * loudness
    return jnp.minimum(jnp.maximum(values, -reach), reach).astype(kind)


def setup_inputs(seed: int = 0) -> dict:
    seeds = jax.random.split(jax.random.key(seed), 6)
    return {
        "hidden_in": gaussian(seeds[0], (TOKENS, D), 1.0, 6.0, ((0, 128),)),
        "lengths": jax.vmap(lambda own: ragged_sizes(own, NSEQ, TOK_GRP, MAXLEN, 2))(jax.random.split(seeds[1], N_GX)).reshape((N_GX, NSEQ)).astype(jnp.int32),
        "attn_norm": jnp.clip(1.0 + 0.1 * jax.random.normal(seeds[2], (D,), jnp.float32), 0.5, 1.5),
        "qkv_weight": gaussian(seeds[3], (D, QKV), D ** -0.5, 0.09375, ((0, 8), (1, 16))),
        "qkv_bias": draw_qkv_bias(jax.random.fold_in(seeds[5], 71), 0),
    }


def norm_rows(values, gain):
    wide = values.astype(jnp.float32)
    scale = lax.rsqrt(lax.optimization_barrier(jnp.mean(wide * wide, axis=1, keepdims=True)) + 1e-06)
    return (wide * scale * gain[None, :]).astype(jnp.bfloat16)

def locate(index, lengths):
    ends = jnp.cumsum(lengths).astype(jnp.int32)
    before = ends[None, :] <= index[:, None]
    segs = lax.optimization_barrier(jnp.sum(before.astype(jnp.int32), axis=1)).astype(jnp.int32)
    begin = lax.optimization_barrier(jnp.sum(jnp.where(before, lengths[None, :], 0), axis=1)).astype(jnp.int32)
    return (segs, (index - begin).astype(jnp.int32))

def rotate(block, pos, heads):
    half = HEAD_DIM // 2
    freqs = 1000000.0 ** (-2.0 * jnp.arange(half, dtype=jnp.float32) / HEAD_DIM)
    angle = pos.astype(jnp.float32)[:, None, None] * freqs[None, None, :]
    wide = block.astype(jnp.float32).reshape(block.shape[0], heads, HEAD_DIM)
    first, second = (wide[..., :half], wide[..., half:])
    turned = jnp.concatenate([first * jnp.cos(angle) - second * jnp.sin(angle), second * jnp.cos(angle) + first * jnp.sin(angle)], axis=2)
    return turned.reshape(block.shape[0], heads * HEAD_DIM).astype(jnp.bfloat16)

def reference(hidden_in, lengths, attn_norm, qkv_weight, qkv_bias):
    normed = norm_rows(hidden_in, attn_norm)
    joined = (jnp.dot(normed, qkv_weight, preferred_element_type=jnp.float32) + qkv_bias[None, :]).astype(jnp.bfloat16)
    qdim = HEADS * HEAD_DIM
    kdim = KV_HEADS * HEAD_DIM
    group = HEADS // KV_HEADS
    scale = 1.0 / HEAD_DIM ** 0.5
    qblock = math.gcd(256, TOK_GRP)
    blocks = TOK_GRP // qblock
    index = jnp.arange(TOK_GRP, dtype=jnp.int32)

    def one_pack(items):
        pack, row_lengths = items
        segs, pos = locate(index, row_lengths)
        queries = rotate(pack[:, :qdim], pos, HEADS)
        keys = rotate(pack[:, qdim:qdim + kdim], pos, KV_HEADS)
        values = pack[:, qdim + kdim:]
        kv_pack = jnp.concatenate([keys, values], axis=1)
        key_wide = keys.astype(jnp.float32).reshape(TOK_GRP, KV_HEADS, HEAD_DIM)
        value_wide = values.astype(jnp.float32).reshape(TOK_GRP, KV_HEADS, HEAD_DIM)

        def one_block(parts):
            qrows, trows, srows = parts
            qwide = qrows.astype(jnp.float32).reshape(qblock, KV_HEADS, group, HEAD_DIM)
            scores = jnp.einsum('rgho,ngo->ghrn', qwide, key_wide) * scale
            allowed = (srows[:, None] == segs[None, :]) & (index[None, :] <= trows[:, None])
            top = lax.optimization_barrier(jnp.max(jnp.where(allowed, scores, -1e+30), axis=3))
            weights = jnp.where(allowed, jnp.exp(scores - top[..., None]), 0.0)
            total = lax.optimization_barrier(jnp.sum(weights, axis=3))
            rounded = lax.optimization_barrier(weights.astype(jnp.bfloat16)).astype(jnp.float32)
            mixed = jnp.einsum('ghrn,ngo->ghro', rounded, value_wide) / total[..., None]
            return jnp.transpose(mixed, (2, 0, 1, 3)).reshape(qblock, qdim).astype(jnp.bfloat16)
        attn_pack = lax.map(one_block, (queries.reshape(blocks, qblock, qdim), index.reshape(blocks, qblock), segs.reshape(blocks, qblock))).reshape(TOK_GRP, qdim)
        return (attn_pack, kv_pack)
    attn, kv_rows = lax.map(one_pack, (joined.reshape(N_GX, TOK_GRP, QKV), lengths))
    attn = attn.reshape(TOKENS, qdim)
    kv_rows = kv_rows.reshape(TOKENS, 2 * kdim)
    return (attn, kv_rows)
```

```python
import math

import jax
import jax.numpy as jnp
from jax import lax
from jax.sharding import PartitionSpec as P
from jax.experimental import pallas as pl
from jax.experimental.pallas import tpu as pltpu

HEADS = 28
KV_HEADS = 4
HEAD_DIM = 128


BLOCK = 256


def flash_body(meta, q_ref, k_ref, v_ref, o_ref, m_ref, l_ref, acc_ref):
    step = pl.program_id(1)
    last = pl.num_programs(1) - 1
    first = meta[4] * BLOCK
    block = jnp.minimum(meta[5] + step, meta[4])
    group = HEADS // KV_HEADS

    @pl.when(step == 0)
    def _():
        m_ref[...] = jnp.full(m_ref.shape, -1e30, jnp.float32)
        l_ref[...] = jnp.zeros(l_ref.shape, jnp.float32)
        acc_ref[...] = jnp.zeros(acc_ref.shape, jnp.float32)

    @pl.when(meta[5] + step <= meta[4])
    def _():
        qrow = first + lax.broadcasted_iota(jnp.int32, (BLOCK, BLOCK), 0)
        kcol = block * BLOCK + lax.broadcasted_iota(jnp.int32, (BLOCK, BLOCK), 1)
        qstart = jnp.zeros((BLOCK, BLOCK), jnp.int32)
        for s in range(4):
            end = meta[s]
            qstart = jnp.where(end <= qrow, end, qstart)
        allowed = (kcol >= qstart) & (kcol <= qrow)
        keys = k_ref[...]
        values = v_ref[...]
        scale = 1.0 / HEAD_DIM**0.5
        for h in range(group):
            q = q_ref[:, h * HEAD_DIM : (h + 1) * HEAD_DIM]
            scores = (
                lax.dot_general(
                    q, keys, (((1,), (1,)), ((), ())), preferred_element_type=jnp.float32
                )
                * scale
            )
            m_prev = m_ref[h][:, :1]
            m_cur = jnp.max(jnp.where(allowed, scores, -1e30), axis=1, keepdims=True)
            m_new = jnp.maximum(m_prev, m_cur)
            shrink = jnp.exp(m_prev - m_new)
            weights = jnp.where(allowed, jnp.exp(scores - m_new), 0.0)
            l_new = l_ref[h][:, :1] * shrink + jnp.sum(weights, axis=1, keepdims=True)
            acc_ref[h] = acc_ref[h] * shrink + jnp.dot(
                weights.astype(jnp.bfloat16), values, preferred_element_type=jnp.float32
            )
            m_ref[h] = jnp.broadcast_to(m_new, (BLOCK, HEAD_DIM))
            l_ref[h] = jnp.broadcast_to(l_new, (BLOCK, HEAD_DIM))

    @pl.when(step == last)
    def _():
        for h in range(group):
            o_ref[:, h * HEAD_DIM : (h + 1) * HEAD_DIM] = (
                acc_ref[h] / l_ref[h][:, :1]
            ).astype(o_ref.dtype)


def flash(meta, queries, kv_all, steps):
    rows = queries.shape[0]
    group = HEADS // KV_HEADS
    width = group * HEAD_DIM

    def key_map(g, t, meta):
        return (jnp.minimum(meta[5] + t, meta[4]), g)

    def value_map(g, t, meta):
        return (jnp.minimum(meta[5] + t, meta[4]), KV_HEADS + g)

    spec = pltpu.PrefetchScalarGridSpec(
        num_scalar_prefetch=1,
        grid=(KV_HEADS, steps),
        in_specs=[
            pl.BlockSpec((rows, width), lambda g, t, meta: (0, g)),
            pl.BlockSpec((BLOCK, HEAD_DIM), key_map),
            pl.BlockSpec((BLOCK, HEAD_DIM), value_map),
        ],
        out_specs=pl.BlockSpec((rows, width), lambda g, t, meta: (0, g)),
        scratch_shapes=[
            pltpu.VMEM((group, rows, HEAD_DIM), jnp.float32),
            pltpu.VMEM((group, rows, HEAD_DIM), jnp.float32),
            pltpu.VMEM((group, rows, HEAD_DIM), jnp.float32),
        ],
    )
    return pl.pallas_call(
        flash_body,
        grid_spec=spec,
        out_shape=jax.ShapeDtypeStruct((rows, HEADS * HEAD_DIM), jnp.bfloat16),
        compiler_params=pltpu.CompilerParams(dimension_semantics=("arbitrary", "arbitrary")),
    )(meta, queries, kv_all, kv_all)


def norm_rows(values, gain):
    wide = values.astype(jnp.float32)
    scale = lax.rsqrt(jnp.mean(wide * wide, axis=1, keepdims=True) + 1e-06)
    return (wide * scale * gain[None, :]).astype(jnp.bfloat16)


def segment_of(index, ends):
    return jnp.sum((ends[None, :] <= index[:, None]).astype(jnp.int32), axis=1)


def rotate(block, pos, heads):
    half = HEAD_DIM // 2
    freqs = 1000000.0 ** (-2.0 * jnp.arange(half, dtype=jnp.float32) / HEAD_DIM)
    angle = pos.astype(jnp.float32)[:, None, None] * freqs[None, None, :]
    wide = block.astype(jnp.float32).reshape(block.shape[0], heads, HEAD_DIM)
    first, second = (wide[..., :half], wide[..., half:])
    turned = jnp.concatenate(
        [
            first * jnp.cos(angle) - second * jnp.sin(angle),
            second * jnp.cos(angle) + first * jnp.sin(angle),
        ],
        axis=2,
    )
    return turned.reshape(block.shape[0], heads * HEAD_DIM).astype(jnp.bfloat16)


def project_joined(normed, weight, bias):
    grouped = lax.all_gather(normed, "gy", axis=0, tiled=True)
    summed = jnp.dot(
        grouped,
        lax.all_gather(weight, "gx", axis=0, tiled=True),
        preferred_element_type=jnp.float32,
    )
    width = weight.shape[1]
    bias_block = lax.dynamic_slice_in_dim(bias, lax.axis_index("gy") * width, width, 0)
    block_out = (summed + bias_block[None, :]).astype(jnp.bfloat16)
    return lax.all_to_all(block_out, "gy", split_axis=0, concat_axis=1, tiled=True)


def on_device(hidden_in, lengths, attn_norm, qkv_weight, qkv_bias):
    rows = hidden_in.shape[0]
    first = lax.axis_index("gy") * rows
    row_lengths = lengths[0]
    qdim = HEADS * HEAD_DIM
    kdim = KV_HEADS * HEAD_DIM
    group = HEADS // KV_HEADS
    normed = norm_rows(hidden_in, attn_norm)
    joined = project_joined(normed, qkv_weight, qkv_bias)
    ends = jnp.cumsum(row_lengths)
    tokens_here = first + jnp.arange(rows, dtype=jnp.int32)
    before = ends[None, :] <= tokens_here[:, None]
    seg_here = jnp.sum(before.astype(jnp.int32), axis=1)
    begin = jnp.sum(jnp.where(before, row_lengths[None, :], 0), axis=1)
    pos = tokens_here - begin
    queries = rotate(joined[:, :qdim], pos, HEADS).reshape(rows, KV_HEADS, group, HEAD_DIM)
    keys = rotate(joined[:, qdim : qdim + kdim], pos, KV_HEADS)
    kv_rows = jnp.concatenate([keys, joined[:, qdim + kdim :]], axis=1)
    piece = lax.all_gather(kv_rows, "gy", axis=0, tiled=True)
    lead = jnp.max(jnp.where(ends <= first, ends, 0))
    meta = jnp.concatenate(
        [ends, jnp.stack([lax.axis_index("gy"), lead // BLOCK, 0, 0]).astype(jnp.int32)]
    ).astype(jnp.int32)
    steps = min(piece.shape[0] // BLOCK, 9)
    attn = flash(meta, queries.reshape(rows, qdim), piece, steps)
    return (attn, kv_rows)


def solution(mesh):
    placed = (P(("gx", "gy"), None), P("gx", None), P(), P("gx", "gy"), P())
    return jax.shard_map(
        on_device,
        mesh=mesh,
        in_specs=placed,
        out_specs=(P(("gx", "gy"), None), P(("gx", "gy"), None)),
        check_vma=False,
    )
```

```python
import math

import jax
import jax.numpy as jnp
from jax import lax
from jax.sharding import PartitionSpec as P
from jax.experimental import pallas as pl
from jax.experimental.pallas import tpu as pltpu

HEADS = 28
KV_HEADS = 4
HEAD_DIM = 128


BLOCK = 256


def flash_body(meta, q_ref, k_ref, v_ref, o_ref, m_ref, l_ref, acc_ref):
    step = pl.program_id(1)
    last = pl.num_programs(1) - 1
    first = meta[4] * BLOCK
    block = jnp.minimum(meta[5] + step, meta[4])
    group = HEADS // KV_HEADS

    @pl.when(step == 0)
    def _():
        m_ref[...] = jnp.full(m_ref.shape, -1e30, jnp.float32)
        l_ref[...] = jnp.zeros(l_ref.shape, jnp.float32)
        acc_ref[...] = jnp.zeros(acc_ref.shape, jnp.float32)

    @pl.when(meta[5] + step <= meta[4])
    def _():
        qrow = first + lax.broadcasted_iota(jnp.int32, (BLOCK, BLOCK), 0)
        kcol = block * BLOCK + lax.broadcasted_iota(jnp.int32, (BLOCK, BLOCK), 1)
        qstart = jnp.zeros((BLOCK, BLOCK), jnp.int32)
        for s in range(4):
            end = meta[s]
            qstart = jnp.where(end <= qrow, end, qstart)
        allowed = (kcol >= qstart) & (kcol <= qrow)
        keys = k_ref[...]
        values = v_ref[...]
        scale = 1.0 / HEAD_DIM**0.5
        for h in range(group):
            q = q_ref[:, h * HEAD_DIM : (h + 1) * HEAD_DIM]
            scores = (
                lax.dot_general(
                    q, keys, (((1,), (1,)), ((), ())), preferred_element_type=jnp.float32
                )
                * scale
            )
            m_prev = m_ref[h][:, :1]
            m_cur = jnp.max(jnp.where(allowed, scores, -1e30), axis=1, keepdims=True)
            m_new = jnp.maximum(m_prev, m_cur)
            shrink = jnp.exp(m_prev - m_new)
            weights = jnp.where(allowed, jnp.exp(scores - m_new), 0.0)
            l_new = l_ref[h][:, :1] * shrink + jnp.sum(weights, axis=1, keepdims=True)
            acc_ref[h] = acc_ref[h] * shrink + jnp.dot(
                weights.astype(jnp.bfloat16), values, preferred_element_type=jnp.float32
            )
            m_ref[h] = jnp.broadcast_to(m_new, (BLOCK, HEAD_DIM))
            l_ref[h] = jnp.broadcast_to(l_new, (BLOCK, HEAD_DIM))

    @pl.when(step == last)
    def _():
        for h in range(group):
            o_ref[:, h * HEAD_DIM : (h + 1) * HEAD_DIM] = (
                acc_ref[h] / l_ref[h][:, :1]
            ).astype(o_ref.dtype)


def flash(meta, queries, kv_all, steps):
    rows = queries.shape[0]
    group = HEADS // KV_HEADS
    width = group * HEAD_DIM

    def key_map(g, t, meta):
        return (jnp.minimum(meta[5] + t, meta[4]), g)

    def value_map(g, t, meta):
        return (jnp.minimum(meta[5] + t, meta[4]), KV_HEADS + g)

    spec = pltpu.PrefetchScalarGridSpec(
        num_scalar_prefetch=1,
        grid=(KV_HEADS, steps),
        in_specs=[
            pl.BlockSpec((rows, width), lambda g, t, meta: (0, g)),
            pl.BlockSpec((BLOCK, HEAD_DIM), key_map),
            pl.BlockSpec((BLOCK, HEAD_DIM), value_map),
        ],
        out_specs=pl.BlockSpec((rows, width), lambda g, t, meta: (0, g)),
        scratch_shapes=[
            pltpu.VMEM((group, rows, HEAD_DIM), jnp.float32),
            pltpu.VMEM((group, rows, HEAD_DIM), jnp.float32),
            pltpu.VMEM((group, rows, HEAD_DIM), jnp.float32),
        ],
    )
    return pl.pallas_call(
        flash_body,
        grid_spec=spec,
        out_shape=jax.ShapeDtypeStruct((rows, HEADS * HEAD_DIM), jnp.bfloat16),
        compiler_params=pltpu.CompilerParams(dimension_semantics=("arbitrary", "arbitrary")),
    )(meta, queries, kv_all, kv_all)


def norm_rows(values, gain):
    wide = values.astype(jnp.float32)
    scale = lax.rsqrt(jnp.mean(wide * wide, axis=1, keepdims=True) + 1e-06)
    return (wide * scale * gain[None, :]).astype(jnp.bfloat16)


def segment_of(index, ends):
    return jnp.sum((ends[None, :] <= index[:, None]).astype(jnp.int32), axis=1)


def rotate(block, pos, heads):
    half = HEAD_DIM // 2
    freqs = 1000000.0 ** (-2.0 * jnp.arange(half, dtype=jnp.float32) / HEAD_DIM)
    angle = pos.astype(jnp.float32)[:, None, None] * freqs[None, None, :]
    wide = block.astype(jnp.float32).reshape(block.shape[0], heads, HEAD_DIM)
    first, second = (wide[..., :half], wide[..., half:])
    turned = jnp.concatenate(
        [
            first * jnp.cos(angle) - second * jnp.sin(angle),
            second * jnp.cos(angle) + first * jnp.sin(angle),
        ],
        axis=2,
    )
    return turned.reshape(block.shape[0], heads * HEAD_DIM).astype(jnp.bfloat16)


def project_joined(normed, weight, bias):
    rows, width = normed.shape[0], weight.shape[1]
    n_x = lax.axis_size("x")
    n_y = lax.axis_size("y")
    grouped = lax.all_gather(normed, "x", axis=0, tiled=True)
    pieces = lax.all_gather(weight, ("z", "c", "y"), axis=0, tiled=False)
    pieces = pieces.reshape(-1, n_y, weight.shape[0], width)
    summed = jnp.einsum(
        "tie,iyec->tyc",
        grouped.reshape(grouped.shape[0], pieces.shape[0], weight.shape[0]),
        pieces,
        preferred_element_type=jnp.float32,
    )
    bias_block = bias.reshape(n_y, n_x, width)
    bias_block = lax.dynamic_index_in_dim(bias_block, lax.axis_index("x"), 1, keepdims=False)
    block_out = (summed + bias_block[None]).astype(jnp.bfloat16)
    swapped = lax.all_to_all(block_out, "x", split_axis=0, concat_axis=1, tiled=True)
    swapped = swapped.reshape(rows, n_x, n_y, width)
    return jnp.transpose(swapped, (0, 2, 1, 3)).reshape(rows, n_y * n_x * width)


def on_device(hidden_in, lengths, attn_norm, qkv_weight, qkv_bias):
    rows = hidden_in.shape[0]
    gy_index = lax.axis_index("y") * lax.axis_size("x") + lax.axis_index("x")
    first = gy_index * rows
    row_lengths = lengths[0]
    qdim = HEADS * HEAD_DIM
    kdim = KV_HEADS * HEAD_DIM
    group = HEADS // KV_HEADS
    normed = norm_rows(hidden_in, attn_norm)
    joined = project_joined(normed, qkv_weight, qkv_bias)
    ends = jnp.cumsum(row_lengths)
    tokens_here = first + jnp.arange(rows, dtype=jnp.int32)
    before = ends[None, :] <= tokens_here[:, None]
    seg_here = jnp.sum(before.astype(jnp.int32), axis=1)
    begin = jnp.sum(jnp.where(before, row_lengths[None, :], 0), axis=1)
    pos = tokens_here - begin
    queries = rotate(joined[:, :qdim], pos, HEADS).reshape(rows, KV_HEADS, group, HEAD_DIM)
    keys = rotate(joined[:, qdim : qdim + kdim], pos, KV_HEADS)
    kv_rows = jnp.concatenate([keys, joined[:, qdim + kdim :]], axis=1)
    piece = lax.all_gather(kv_rows, ("y", "x"), axis=0, tiled=True)
    lead = jnp.max(jnp.where(ends <= first, ends, 0))
    meta = jnp.concatenate(
        [ends, jnp.stack([gy_index, lead // BLOCK, 0, 0]).astype(jnp.int32)]
    ).astype(jnp.int32)
    steps = min(piece.shape[0] // BLOCK, 9)
    attn = flash(meta, queries.reshape(rows, qdim), piece, steps)
    return (attn, kv_rows)


def solution(mesh):
    n_z = len({d.coords[2] for d in mesh.devices.flat})
    grid = mesh.devices.reshape(n_z, -1, *mesh.devices.shape[1:])
    n_y = len({d.coords[1] for d in mesh.devices.flat})
    grid = grid.reshape(grid.shape[0], grid.shape[1], n_y, -1)
    split = jax.sharding.Mesh(grid, ("z", "c", "y", "x"))
    tokens = P(("z", "c", "y", "x"), None)
    placed = (tokens, P(("z", "c"), None), P(), P(("z", "c"), ("y", "x")), P())
    return jax.shard_map(
        on_device,
        mesh=split,
        in_specs=placed,
        out_specs=(tokens, tokens),
        check_vma=False,
    )
```

```python
import math

import jax
import jax.numpy as jnp
from jax import lax
from jax.sharding import PartitionSpec as P
from jax.experimental import pallas as pl
from jax.experimental.pallas import tpu as pltpu

HEADS = 28
KV_HEADS = 4
HEAD_DIM = 128
MAXLEN = 2048


BLOCK = 256


def flash_body(meta, q_ref, k_ref, v_ref, o_ref, m_ref, l_ref, acc_ref):
    step = pl.program_id(1)
    last = pl.num_programs(1) - 1
    first = meta[4] * BLOCK
    block = jnp.minimum(meta[5] + step, meta[4])
    group = HEADS // KV_HEADS

    @pl.when(step == 0)
    def _():
        m_ref[...] = jnp.full(m_ref.shape, -1e30, jnp.float32)
        l_ref[...] = jnp.zeros(l_ref.shape, jnp.float32)
        acc_ref[...] = jnp.zeros(acc_ref.shape, jnp.float32)

    @pl.when(meta[5] + step <= meta[4])
    def _():
        qrow = first + lax.broadcasted_iota(jnp.int32, (BLOCK, BLOCK), 0)
        kcol = block * BLOCK + lax.broadcasted_iota(jnp.int32, (BLOCK, BLOCK), 1)
        qstart = jnp.zeros((BLOCK, BLOCK), jnp.int32)
        for s in range(4):
            end = meta[s]
            qstart = jnp.where(end <= qrow, end, qstart)
        allowed = (kcol >= qstart) & (kcol <= qrow)
        keys = k_ref[...]
        values = v_ref[...]
        scale = 1.0 / HEAD_DIM**0.5
        for h in range(group):
            q = q_ref[:, h * HEAD_DIM : (h + 1) * HEAD_DIM]
            scores = (
                lax.dot_general(
                    q, keys, (((1,), (1,)), ((), ())), preferred_element_type=jnp.float32
                )
                * scale
            )
            m_prev = m_ref[h][:, :1]
            m_cur = jnp.max(jnp.where(allowed, scores, -1e30), axis=1, keepdims=True)
            m_new = jnp.maximum(m_prev, m_cur)
            shrink = jnp.exp(m_prev - m_new)
            weights = jnp.where(allowed, jnp.exp(scores - m_new), 0.0)
            l_new = l_ref[h][:, :1] * shrink + jnp.sum(weights, axis=1, keepdims=True)
            acc_ref[h] = acc_ref[h] * shrink + jnp.dot(
                weights.astype(jnp.bfloat16), values, preferred_element_type=jnp.float32
            )
            m_ref[h] = jnp.broadcast_to(m_new, (BLOCK, HEAD_DIM))
            l_ref[h] = jnp.broadcast_to(l_new, (BLOCK, HEAD_DIM))

    @pl.when(step == last)
    def _():
        for h in range(group):
            o_ref[:, h * HEAD_DIM : (h + 1) * HEAD_DIM] = (
                acc_ref[h] / l_ref[h][:, :1]
            ).astype(o_ref.dtype)


def flash(meta, queries, kv_all, steps):
    rows = queries.shape[0]
    group = HEADS // KV_HEADS
    width = group * HEAD_DIM

    def key_map(g, t, meta):
        return (jnp.minimum(meta[5] + t, meta[4]) - meta[4] + steps - 1, g)

    def value_map(g, t, meta):
        return (jnp.minimum(meta[5] + t, meta[4]) - meta[4] + steps - 1, KV_HEADS + g)

    spec = pltpu.PrefetchScalarGridSpec(
        num_scalar_prefetch=1,
        grid=(KV_HEADS, steps),
        in_specs=[
            pl.BlockSpec((rows, width), lambda g, t, meta: (0, g)),
            pl.BlockSpec((BLOCK, HEAD_DIM), key_map),
            pl.BlockSpec((BLOCK, HEAD_DIM), value_map),
        ],
        out_specs=pl.BlockSpec((rows, width), lambda g, t, meta: (0, g)),
        scratch_shapes=[
            pltpu.VMEM((group, rows, HEAD_DIM), jnp.float32),
            pltpu.VMEM((group, rows, HEAD_DIM), jnp.float32),
            pltpu.VMEM((group, rows, HEAD_DIM), jnp.float32),
        ],
    )
    return pl.pallas_call(
        flash_body,
        grid_spec=spec,
        out_shape=jax.ShapeDtypeStruct((rows, HEADS * HEAD_DIM), jnp.bfloat16),
        compiler_params=pltpu.CompilerParams(dimension_semantics=("arbitrary", "arbitrary")),
    )(meta, queries, kv_all, kv_all)


def norm_rows(values, gain):
    wide = values.astype(jnp.float32)
    scale = lax.rsqrt(jnp.mean(wide * wide, axis=1, keepdims=True) + 1e-06)
    return (wide * scale * gain[None, :]).astype(jnp.bfloat16)


def segment_of(index, ends):
    return jnp.sum((ends[None, :] <= index[:, None]).astype(jnp.int32), axis=1)


def rotate(block, pos, heads):
    half = HEAD_DIM // 2
    freqs = 1000000.0 ** (-2.0 * jnp.arange(half, dtype=jnp.float32) / HEAD_DIM)
    angle = pos.astype(jnp.float32)[:, None, None] * freqs[None, None, :]
    wide = block.astype(jnp.float32).reshape(block.shape[0], heads, HEAD_DIM)
    first, second = (wide[..., :half], wide[..., half:])
    turned = jnp.concatenate(
        [
            first * jnp.cos(angle) - second * jnp.sin(angle),
            second * jnp.cos(angle) + first * jnp.sin(angle),
        ],
        axis=2,
    )
    return turned.reshape(block.shape[0], heads * HEAD_DIM).astype(jnp.bfloat16)


def project_joined(normed, weight, bias):
    rows, width = normed.shape[0], weight.shape[1]
    n_x = lax.axis_size("x")
    n_y = lax.axis_size("y")
    grouped = lax.all_gather(normed, "x", axis=0, tiled=True)
    pieces = lax.all_gather(weight, ("z", "c", "y"), axis=0, tiled=False)
    pieces = pieces.reshape(-1, n_y, weight.shape[0], width)
    summed = jnp.einsum(
        "tie,iyec->tyc",
        grouped.reshape(grouped.shape[0], pieces.shape[0], weight.shape[0]),
        pieces,
        preferred_element_type=jnp.float32,
    )
    bias_block = bias.reshape(n_y, n_x, width)
    bias_block = lax.dynamic_index_in_dim(bias_block, lax.axis_index("x"), 1, keepdims=False)
    block_out = (summed + bias_block[None]).astype(jnp.bfloat16)
    swapped = lax.all_to_all(block_out, "x", split_axis=0, concat_axis=1, tiled=True)
    swapped = swapped.reshape(rows, n_x, n_y, width)
    return jnp.transpose(swapped, (0, 2, 1, 3)).reshape(rows, n_y * n_x * width)


def on_device(hidden_in, lengths, attn_norm, qkv_weight, qkv_bias):
    rows = hidden_in.shape[0]
    gy_index = lax.axis_index("y") * lax.axis_size("x") + lax.axis_index("x")
    first = gy_index * rows
    row_lengths = lengths[0]
    qdim = HEADS * HEAD_DIM
    kdim = KV_HEADS * HEAD_DIM
    group = HEADS // KV_HEADS
    normed = norm_rows(hidden_in, attn_norm)
    joined = project_joined(normed, qkv_weight, qkv_bias)
    ends = jnp.cumsum(row_lengths)
    tokens_here = first + jnp.arange(rows, dtype=jnp.int32)
    before = ends[None, :] <= tokens_here[:, None]
    seg_here = jnp.sum(before.astype(jnp.int32), axis=1)
    begin = jnp.sum(jnp.where(before, row_lengths[None, :], 0), axis=1)
    pos = tokens_here - begin
    queries = rotate(joined[:, :qdim], pos, HEADS).reshape(rows, KV_HEADS, group, HEAD_DIM)
    keys = rotate(joined[:, qdim : qdim + kdim], pos, KV_HEADS)
    kv_rows = jnp.concatenate([keys, joined[:, qdim + kdim :]], axis=1)
    n_gy = lax.axis_size("y") * lax.axis_size("x")
    reach = min(n_gy - 1, (MAXLEN - 1) // rows + 1)
    window = []
    for back in range(reach, 0, -1):
        pairs = [(s, s + back) for s in range(n_gy - back)]
        window.append(lax.ppermute(kv_rows, ("y", "x"), pairs))
    piece = jnp.concatenate(window + [kv_rows], axis=0)
    lead = jnp.max(jnp.where(ends <= first, ends, 0))
    meta = jnp.concatenate(
        [ends, jnp.stack([gy_index, lead // BLOCK, 0, 0]).astype(jnp.int32)]
    ).astype(jnp.int32)
    attn = flash(meta, queries.reshape(rows, qdim), piece, reach + 1)
    return (attn, kv_rows)


def solution(mesh):
    n_z = len({d.coords[2] for d in mesh.devices.flat})
    grid = mesh.devices.reshape(n_z, -1, *mesh.devices.shape[1:])
    n_y = len({d.coords[1] for d in mesh.devices.flat})
    grid = grid.reshape(grid.shape[0], grid.shape[1], n_y, -1)
    split = jax.sharding.Mesh(grid, ("z", "c", "y", "x"))
    tokens = P(("z", "c", "y", "x"), None)
    placed = (tokens, P(("z", "c"), None), P(), P(("z", "c"), ("y", "x")), P())
    return jax.shard_map(
        on_device,
        mesh=split,
        in_specs=placed,
        out_specs=(tokens, tokens),
        check_vma=False,
    )
```

```python
import math

import jax
import jax.numpy as jnp
from jax import lax
from jax.sharding import PartitionSpec as P
from jax.experimental import pallas as pl
from jax.experimental.pallas import tpu as pltpu

HEADS = 28
KV_HEADS = 4
HEAD_DIM = 128


BLOCK = 256


LANES = 128


def flash_body(meta, q_ref, k_ref, v_ref, o_ref, bias_ref, m_ref, l_ref, acc_ref):
    step = pl.program_id(1)
    last = pl.num_programs(1) - 1
    first = meta[4] * BLOCK
    block = jnp.minimum(meta[5] + step, meta[4])
    group = HEADS // KV_HEADS

    @pl.when(step == 0)
    def _():
        m_ref[...] = jnp.full(m_ref.shape, -1e30, jnp.float32)
        l_ref[...] = jnp.zeros(l_ref.shape, jnp.float32)
        acc_ref[...] = jnp.zeros(acc_ref.shape, jnp.float32)

    @pl.when(meta[5] + step <= meta[4])
    def _():
        krow = block * BLOCK + lax.broadcasted_iota(jnp.int32, (BLOCK, 1), 0)
        qcol = first + lax.broadcasted_iota(jnp.int32, (1, BLOCK), 1)
        qstart = jnp.zeros((1, BLOCK), jnp.int32)
        for s in range(4):
            end = meta[s]
            qstart = jnp.where(end <= qcol, end, qstart)
        allowed = (krow >= qstart) & (krow <= qcol)
        bias_ref[...] = jnp.where(allowed, 0.0, -1e30).astype(jnp.float32)
        keys = k_ref[...]
        values = v_ref[...]
        scale = 1.0 / HEAD_DIM**0.5
        for h in range(group):
            heads = slice(h * HEAD_DIM, (h + 1) * HEAD_DIM)
            for c in range(BLOCK // LANES):
                cols = slice(c * LANES, (c + 1) * LANES)
                q = q_ref[heads, cols]
                scores = (
                    jnp.dot(keys, q, preferred_element_type=jnp.float32) * scale
                    + bias_ref[:, cols]
                )
                m_prev = m_ref[h, :, cols]
                m_new = jnp.maximum(m_prev, jnp.max(scores, axis=0, keepdims=True))
                shrink = jnp.exp(m_prev - m_new)
                weights = jnp.exp(scores - m_new)
                l_ref[h, :, cols] = l_ref[h, :, cols] * shrink + jnp.sum(
                    weights, axis=0, keepdims=True
                )
                acc_ref[h, :, cols] = acc_ref[h, :, cols] * shrink + jnp.dot(
                    values, weights.astype(jnp.bfloat16), preferred_element_type=jnp.float32
                )
                m_ref[h, :, cols] = m_new

    @pl.when(step == last)
    def _():
        for h in range(group):
            o_ref[h * HEAD_DIM : (h + 1) * HEAD_DIM, :] = (acc_ref[h] / l_ref[h]).astype(
                o_ref.dtype
            )


def flash(meta, queries_t, keys, values_t, steps):
    rows = queries_t.shape[1]
    group = HEADS // KV_HEADS
    width = group * HEAD_DIM

    def key_map(g, t, meta):
        return (jnp.minimum(meta[5] + t, meta[4]), g)

    def value_map(g, t, meta):
        return (g, jnp.minimum(meta[5] + t, meta[4]))

    spec = pltpu.PrefetchScalarGridSpec(
        num_scalar_prefetch=1,
        grid=(KV_HEADS, steps),
        in_specs=[
            pl.BlockSpec((width, rows), lambda g, t, meta: (g, 0)),
            pl.BlockSpec((BLOCK, HEAD_DIM), key_map),
            pl.BlockSpec((HEAD_DIM, BLOCK), value_map),
        ],
        out_specs=pl.BlockSpec((width, rows), lambda g, t, meta: (g, 0)),
        scratch_shapes=[
            pltpu.VMEM((BLOCK, rows), jnp.float32),
            pltpu.VMEM((group, 1, rows), jnp.float32),
            pltpu.VMEM((group, 1, rows), jnp.float32),
            pltpu.VMEM((group, HEAD_DIM, rows), jnp.float32),
        ],
    )
    return pl.pallas_call(
        flash_body,
        grid_spec=spec,
        out_shape=jax.ShapeDtypeStruct((HEADS * HEAD_DIM, rows), jnp.bfloat16),
        compiler_params=pltpu.CompilerParams(dimension_semantics=("arbitrary", "arbitrary")),
    )(meta, queries_t, keys, values_t)


def norm_rows(values, gain):
    wide = values.astype(jnp.float32)
    scale = lax.rsqrt(jnp.mean(wide * wide, axis=1, keepdims=True) + 1e-06)
    return (wide * scale * gain[None, :]).astype(jnp.bfloat16)


def segment_of(index, ends):
    return jnp.sum((ends[None, :] <= index[:, None]).astype(jnp.int32), axis=1)


def rotate(block, pos, heads):
    half = HEAD_DIM // 2
    freqs = 1000000.0 ** (-2.0 * jnp.arange(half, dtype=jnp.float32) / HEAD_DIM)
    angle = pos.astype(jnp.float32)[:, None, None] * freqs[None, None, :]
    wide = block.astype(jnp.float32).reshape(block.shape[0], heads, HEAD_DIM)
    first, second = (wide[..., :half], wide[..., half:])
    turned = jnp.concatenate(
        [
            first * jnp.cos(angle) - second * jnp.sin(angle),
            second * jnp.cos(angle) + first * jnp.sin(angle),
        ],
        axis=2,
    )
    return turned.reshape(block.shape[0], heads * HEAD_DIM).astype(jnp.bfloat16)


def project_joined(normed, weight, bias):
    rows, width = normed.shape[0], weight.shape[1]
    n_x = lax.axis_size("x")
    n_y = lax.axis_size("y")
    grouped = lax.all_gather(normed, "x", axis=0, tiled=True)
    pieces = lax.all_gather(weight, ("z", "c", "y"), axis=0, tiled=False)
    pieces = pieces.reshape(-1, n_y, weight.shape[0], width)
    summed = jnp.einsum(
        "tie,iyec->tyc",
        grouped.reshape(grouped.shape[0], pieces.shape[0], weight.shape[0]),
        pieces,
        preferred_element_type=jnp.float32,
    )
    bias_block = bias.reshape(n_y, n_x, width)
    bias_block = lax.dynamic_index_in_dim(bias_block, lax.axis_index("x"), 1, keepdims=False)
    block_out = (summed + bias_block[None]).astype(jnp.bfloat16)
    swapped = lax.all_to_all(block_out, "x", split_axis=0, concat_axis=1, tiled=True)
    swapped = swapped.reshape(rows, n_x, n_y, width)
    return jnp.transpose(swapped, (0, 2, 1, 3)).reshape(rows, n_y * n_x * width)


def on_device(hidden_in, lengths, attn_norm, qkv_weight, qkv_bias):
    rows = hidden_in.shape[0]
    gy_index = lax.axis_index("y") * lax.axis_size("x") + lax.axis_index("x")
    first = gy_index * rows
    row_lengths = lengths[0]
    qdim = HEADS * HEAD_DIM
    kdim = KV_HEADS * HEAD_DIM
    group = HEADS // KV_HEADS
    normed = norm_rows(hidden_in, attn_norm)
    joined = project_joined(normed, qkv_weight, qkv_bias)
    ends = jnp.cumsum(row_lengths)
    tokens_here = first + jnp.arange(rows, dtype=jnp.int32)
    before = ends[None, :] <= tokens_here[:, None]
    seg_here = jnp.sum(before.astype(jnp.int32), axis=1)
    begin = jnp.sum(jnp.where(before, row_lengths[None, :], 0), axis=1)
    pos = tokens_here - begin
    queries = rotate(joined[:, :qdim], pos, HEADS).reshape(rows, KV_HEADS, group, HEAD_DIM)
    keys = rotate(joined[:, qdim : qdim + kdim], pos, KV_HEADS)
    kv_rows = jnp.concatenate([keys, joined[:, qdim + kdim :]], axis=1)
    piece = lax.all_gather(kv_rows, ("y", "x"), axis=0, tiled=True)
    lead = jnp.max(jnp.where(ends <= first, ends, 0))
    meta = jnp.concatenate(
        [ends, jnp.stack([gy_index, lead // BLOCK, 0, 0]).astype(jnp.int32)]
    ).astype(jnp.int32)
    steps = min(piece.shape[0] // BLOCK, 9)
    queries_t = jnp.transpose(queries.reshape(rows, qdim))
    values_t = jnp.transpose(piece[:, kdim:])
    attn = jnp.transpose(flash(meta, queries_t, piece[:, :kdim], values_t, steps))
    return (attn, kv_rows)


def solution(mesh):
    n_z = len({d.coords[2] for d in mesh.devices.flat})
    grid = mesh.devices.reshape(n_z, -1, *mesh.devices.shape[1:])
    n_y = len({d.coords[1] for d in mesh.devices.flat})
    grid = grid.reshape(grid.shape[0], grid.shape[1], n_y, -1)
    split = jax.sharding.Mesh(grid, ("z", "c", "y", "x"))
    tokens = P(("z", "c", "y", "x"), None)
    placed = (tokens, P(("z", "c"), None), P(), P(("z", "c"), ("y", "x")), P())
    return jax.shard_map(
        on_device,
        mesh=split,
        in_specs=placed,
        out_specs=(tokens, tokens),
        check_vma=False,
    )
```

```python
import math

import jax
import jax.numpy as jnp
from jax import lax
from jax.sharding import PartitionSpec as P
from jax.experimental import pallas as pl
from jax.experimental.pallas import tpu as pltpu

HEADS = 28
KV_HEADS = 4
HEAD_DIM = 128


BLOCK = 256


LANES = 128


def flash_body(meta, q_ref, k_ref, v_ref, o_ref, bias_ref, m_ref, l_ref, acc_ref):
    step = pl.program_id(1)
    last = pl.num_programs(1) - 1
    first = meta[4] * BLOCK
    block = jnp.minimum(meta[5] + step, meta[4])
    group = HEADS // KV_HEADS

    @pl.when(step == 0)
    def _():
        m_ref[...] = jnp.full(m_ref.shape, -1e30, jnp.float32)
        l_ref[...] = jnp.zeros(l_ref.shape, jnp.float32)
        acc_ref[...] = jnp.zeros(acc_ref.shape, jnp.float32)

    @pl.when(meta[5] + step <= meta[4])
    def _():
        krow = block * BLOCK + lax.broadcasted_iota(jnp.int32, (BLOCK, 1), 0)
        qcol = first + lax.broadcasted_iota(jnp.int32, (1, BLOCK), 1)
        qstart = jnp.zeros((1, BLOCK), jnp.int32)
        for s in range(4):
            end = meta[s]
            qstart = jnp.where(end <= qcol, end, qstart)
        allowed = (krow >= qstart) & (krow <= qcol)
        bias_ref[...] = jnp.where(allowed, 0.0, -1e30).astype(jnp.float32)
        keys = k_ref[...]
        values = v_ref[...]
        scale = 1.0 / HEAD_DIM**0.5
        for h in range(group):
            heads = slice(h * HEAD_DIM, (h + 1) * HEAD_DIM)
            for c in range(BLOCK // LANES):
                cols = slice(c * LANES, (c + 1) * LANES)
                q = q_ref[heads, cols]
                scores = (
                    jnp.dot(keys, q, preferred_element_type=jnp.float32) * scale
                    + bias_ref[:, cols]
                )
                m_prev = m_ref[h, :, cols]
                m_new = jnp.maximum(m_prev, jnp.max(scores, axis=0, keepdims=True))
                shrink = jnp.exp(m_prev - m_new)
                weights = jnp.exp(scores - m_new)
                l_ref[h, :, cols] = l_ref[h, :, cols] * shrink + jnp.sum(
                    weights, axis=0, keepdims=True
                )
                acc_ref[h, :, cols] = acc_ref[h, :, cols] * shrink + jnp.dot(
                    values, weights.astype(jnp.bfloat16), preferred_element_type=jnp.float32
                )
                m_ref[h, :, cols] = m_new

    @pl.when(step == last)
    def _():
        for h in range(group):
            o_ref[h * HEAD_DIM : (h + 1) * HEAD_DIM, :] = (acc_ref[h] / l_ref[h]).astype(
                o_ref.dtype
            )


def flash(meta, queries_t, keys, values_t, steps):
    rows = queries_t.shape[1]
    group = HEADS // KV_HEADS
    width = group * HEAD_DIM

    def key_map(g, t, meta):
        return (jnp.minimum(meta[5] + t, meta[4]), g)

    def value_map(g, t, meta):
        return (g, jnp.minimum(meta[5] + t, meta[4]))

    spec = pltpu.PrefetchScalarGridSpec(
        num_scalar_prefetch=1,
        grid=(KV_HEADS, steps),
        in_specs=[
            pl.BlockSpec((width, rows), lambda g, t, meta: (g, 0)),
            pl.BlockSpec((BLOCK, HEAD_DIM), key_map),
            pl.BlockSpec((HEAD_DIM, BLOCK), value_map),
        ],
        out_specs=pl.BlockSpec((width, rows), lambda g, t, meta: (g, 0)),
        scratch_shapes=[
            pltpu.VMEM((BLOCK, rows), jnp.float32),
            pltpu.VMEM((group, 1, rows), jnp.float32),
            pltpu.VMEM((group, 1, rows), jnp.float32),
            pltpu.VMEM((group, HEAD_DIM, rows), jnp.float32),
        ],
    )
    return pl.pallas_call(
        flash_body,
        grid_spec=spec,
        out_shape=jax.ShapeDtypeStruct((HEADS * HEAD_DIM, rows), jnp.bfloat16),
        compiler_params=pltpu.CompilerParams(dimension_semantics=("arbitrary", "arbitrary")),
    )(meta, queries_t, keys, values_t)


def norm_rows(values, gain):
    wide = values.astype(jnp.float32)
    scale = lax.rsqrt(jnp.mean(wide * wide, axis=1, keepdims=True) + 1e-06)
    return (wide * scale * gain[None, :]).astype(jnp.bfloat16)


def segment_of(index, ends):
    return jnp.sum((ends[None, :] <= index[:, None]).astype(jnp.int32), axis=1)


def rotate(block, pos, heads):
    half = HEAD_DIM // 2
    freqs = 1000000.0 ** (-2.0 * jnp.arange(half, dtype=jnp.float32) / HEAD_DIM)
    angle = pos.astype(jnp.float32)[:, None, None] * freqs[None, None, :]
    wide = block.astype(jnp.float32).reshape(block.shape[0], heads, HEAD_DIM)
    first, second = (wide[..., :half], wide[..., half:])
    turned = jnp.concatenate(
        [
            first * jnp.cos(angle) - second * jnp.sin(angle),
            second * jnp.cos(angle) + first * jnp.sin(angle),
        ],
        axis=2,
    )
    return turned.reshape(block.shape[0], heads * HEAD_DIM).astype(jnp.bfloat16)


def project_joined(normed, weight, bias):
    rows, width = normed.shape[0], weight.shape[1]
    n_x = lax.axis_size("x")
    n_y = lax.axis_size("y")
    here = lax.axis_index("x")
    shifted = [normed]
    for step in range(1, n_x):
        pairs = [(s, (s + step) % n_x) for s in range(n_x)]
        shifted.append(lax.ppermute(normed, "x", pairs))
    slots = jnp.stack(shifted)
    order = (here - jnp.arange(n_x)) % n_x
    grouped = jnp.take(slots, order, axis=0).reshape(n_x * rows, -1)
    pieces = lax.all_gather(weight, ("y", "z", "c"), axis=0, tiled=False)
    pieces = pieces.reshape(n_y, -1, width)
    summed = jnp.einsum(
        "td,ydc->tyc",
        grouped,
        pieces,
        preferred_element_type=jnp.float32,
    )
    bias_block = bias.reshape(n_y, n_x, width)
    bias_block = lax.dynamic_index_in_dim(bias_block, lax.axis_index("x"), 1, keepdims=False)
    block_out = (summed + bias_block[None]).astype(jnp.bfloat16)
    swapped = lax.all_to_all(block_out, "x", split_axis=0, concat_axis=1, tiled=True)
    swapped = swapped.reshape(rows, n_x, n_y, width)
    return jnp.transpose(swapped, (0, 2, 1, 3)).reshape(rows, n_y * n_x * width)


def on_device(hidden_in, lengths, attn_norm, qkv_weight, qkv_bias):
    rows = hidden_in.shape[0]
    gy_index = lax.axis_index("y") * lax.axis_size("x") + lax.axis_index("x")
    first = gy_index * rows
    row_lengths = lengths[0]
    qdim = HEADS * HEAD_DIM
    kdim = KV_HEADS * HEAD_DIM
    group = HEADS // KV_HEADS
    normed = norm_rows(hidden_in, attn_norm)
    joined = project_joined(normed, qkv_weight, qkv_bias)
    ends = jnp.cumsum(row_lengths)
    tokens_here = first + jnp.arange(rows, dtype=jnp.int32)
    before = ends[None, :] <= tokens_here[:, None]
    seg_here = jnp.sum(before.astype(jnp.int32), axis=1)
    begin = jnp.sum(jnp.where(before, row_lengths[None, :], 0), axis=1)
    pos = tokens_here - begin
    queries = rotate(joined[:, :qdim], pos, HEADS).reshape(rows, KV_HEADS, group, HEAD_DIM)
    keys = rotate(joined[:, qdim : qdim + kdim], pos, KV_HEADS)
    kv_rows = jnp.concatenate([keys, joined[:, qdim + kdim :]], axis=1)
    piece = lax.all_gather(kv_rows, ("y", "x"), axis=0, tiled=True)
    lead = jnp.max(jnp.where(ends <= first, ends, 0))
    meta = jnp.concatenate(
        [ends, jnp.stack([gy_index, lead // BLOCK, 0, 0]).astype(jnp.int32)]
    ).astype(jnp.int32)
    steps = min(piece.shape[0] // BLOCK, 9)
    queries_t = jnp.transpose(queries.reshape(rows, qdim))
    values_t = jnp.transpose(piece[:, kdim:])
    attn = jnp.transpose(flash(meta, queries_t, piece[:, :kdim], values_t, steps))
    return (attn, kv_rows)


def solution(mesh):
    n_z = len({d.coords[2] for d in mesh.devices.flat})
    grid = mesh.devices.reshape(n_z, -1, *mesh.devices.shape[1:])
    n_y = len({d.coords[1] for d in mesh.devices.flat})
    grid = grid.reshape(grid.shape[0], grid.shape[1], n_y, -1)
    split = jax.sharding.Mesh(grid, ("z", "c", "y", "x"))
    tokens = P(("z", "c", "y", "x"), None)
    placed = (tokens, P(("z", "c"), None), P(), P(("z", "c"), ("y", "x")), P())
    return jax.shard_map(
        on_device,
        mesh=split,
        in_specs=placed,
        out_specs=(tokens, tokens),
        check_vma=False,
    )
```

```python
import math

import jax
import jax.numpy as jnp
from jax import lax
from jax.sharding import PartitionSpec as P
from jax.experimental import pallas as pl
from jax.experimental.pallas import tpu as pltpu

HEADS = 28
KV_HEADS = 4
HEAD_DIM = 128


BLOCK = 256


LANES = 128


def flash_body(meta, q_ref, k_ref, v_ref, o_ref, bias_ref, m_ref, l_ref, acc_ref):
    step = pl.program_id(1)
    last = pl.num_programs(1) - 1
    first = meta[4] * BLOCK
    block = jnp.minimum(meta[5] + step, meta[4])
    group = HEADS // KV_HEADS

    @pl.when(step == 0)
    def _():
        m_ref[...] = jnp.full(m_ref.shape, -1e30, jnp.float32)
        l_ref[...] = jnp.zeros(l_ref.shape, jnp.float32)
        acc_ref[...] = jnp.zeros(acc_ref.shape, jnp.float32)

    @pl.when(meta[5] + step <= meta[4])
    def _():
        krow = block * BLOCK + lax.broadcasted_iota(jnp.int32, (BLOCK, 1), 0)
        qcol = first + lax.broadcasted_iota(jnp.int32, (1, BLOCK), 1)
        qstart = jnp.zeros((1, BLOCK), jnp.int32)
        for s in range(4):
            end = meta[s]
            qstart = jnp.where(end <= qcol, end, qstart)
        allowed = (krow >= qstart) & (krow <= qcol)
        bias_ref[...] = jnp.where(allowed, 0.0, -1e30).astype(jnp.float32)
        keys = k_ref[...]
        values = v_ref[...]
        scale = 1.0 / HEAD_DIM**0.5
        for h in range(group):
            heads = slice(h * HEAD_DIM, (h + 1) * HEAD_DIM)
            for c in range(BLOCK // LANES):
                cols = slice(c * LANES, (c + 1) * LANES)
                q = q_ref[heads, cols]
                scores = (
                    jnp.dot(keys, q, preferred_element_type=jnp.float32) * scale
                    + bias_ref[:, cols]
                )
                m_prev = m_ref[h, :, cols]
                m_new = jnp.maximum(m_prev, jnp.max(scores, axis=0, keepdims=True))
                shrink = jnp.exp(m_prev - m_new)
                weights = jnp.exp(scores - m_new)
                l_ref[h, :, cols] = l_ref[h, :, cols] * shrink + jnp.sum(
                    weights, axis=0, keepdims=True
                )
                acc_ref[h, :, cols] = acc_ref[h, :, cols] * shrink + jnp.dot(
                    values, weights.astype(jnp.bfloat16), preferred_element_type=jnp.float32
                )
                m_ref[h, :, cols] = m_new

    @pl.when(step == last)
    def _():
        for h in range(group):
            o_ref[h * HEAD_DIM : (h + 1) * HEAD_DIM, :] = (acc_ref[h] / l_ref[h]).astype(
                o_ref.dtype
            )


def flash(meta, queries_t, keys, values_t, steps):
    rows = queries_t.shape[1]
    group = HEADS // KV_HEADS
    width = group * HEAD_DIM

    def key_map(g, t, meta):
        return (jnp.minimum(meta[5] + t, meta[4]), g)

    def value_map(g, t, meta):
        return (g, jnp.minimum(meta[5] + t, meta[4]))

    spec = pltpu.PrefetchScalarGridSpec(
        num_scalar_prefetch=1,
        grid=(KV_HEADS, steps),
        in_specs=[
            pl.BlockSpec((width, rows), lambda g, t, meta: (g, 0)),
            pl.BlockSpec((BLOCK, HEAD_DIM), key_map),
            pl.BlockSpec((HEAD_DIM, BLOCK), value_map),
        ],
        out_specs=pl.BlockSpec((width, rows), lambda g, t, meta: (g, 0)),
        scratch_shapes=[
            pltpu.VMEM((BLOCK, rows), jnp.float32),
            pltpu.VMEM((group, 1, rows), jnp.float32),
            pltpu.VMEM((group, 1, rows), jnp.float32),
            pltpu.VMEM((group, HEAD_DIM, rows), jnp.float32),
        ],
    )
    return pl.pallas_call(
        flash_body,
        grid_spec=spec,
        out_shape=jax.ShapeDtypeStruct((HEADS * HEAD_DIM, rows), jnp.bfloat16),
        compiler_params=pltpu.CompilerParams(dimension_semantics=("arbitrary", "arbitrary")),
    )(meta, queries_t, keys, values_t)


def norm_rows(values, gain):
    wide = values.astype(jnp.float32)
    scale = lax.rsqrt(jnp.mean(wide * wide, axis=1, keepdims=True) + 1e-06)
    return (wide * scale * gain[None, :]).astype(jnp.bfloat16)


def segment_of(index, ends):
    return jnp.sum((ends[None, :] <= index[:, None]).astype(jnp.int32), axis=1)


def rotate(block, pos, heads):
    half = HEAD_DIM // 2
    freqs = 1000000.0 ** (-2.0 * jnp.arange(half, dtype=jnp.float32) / HEAD_DIM)
    angle = pos.astype(jnp.float32)[:, None, None] * freqs[None, None, :]
    wide = block.astype(jnp.float32).reshape(block.shape[0], heads, HEAD_DIM)
    first, second = (wide[..., :half], wide[..., half:])
    turned = jnp.concatenate(
        [
            first * jnp.cos(angle) - second * jnp.sin(angle),
            second * jnp.cos(angle) + first * jnp.sin(angle),
        ],
        axis=2,
    )
    return turned.reshape(block.shape[0], heads * HEAD_DIM).astype(jnp.bfloat16)


def project_joined(normed, weight, bias):
    rows, width = normed.shape[0], weight.shape[1]
    n_x = lax.axis_size("x")
    n_y = lax.axis_size("y")
    here = lax.axis_index("x")
    shifted = [normed]
    for step in range(1, n_x):
        pairs = [(s, (s + step) % n_x) for s in range(n_x)]
        shifted.append(lax.ppermute(normed, "x", pairs))
    grouped = jnp.zeros((n_x * rows, normed.shape[1]), normed.dtype)
    for step, piece in enumerate(shifted):
        at = ((here - step) % n_x) * rows
        grouped = lax.dynamic_update_slice_in_dim(grouped, piece, at, 0)
    pieces = lax.all_gather(weight, ("z", "c", "y"), axis=0, tiled=False)
    pieces = pieces.reshape(-1, n_y, weight.shape[0], width)
    summed = jnp.einsum(
        "tie,iyec->tyc",
        grouped.reshape(grouped.shape[0], pieces.shape[0], weight.shape[0]),
        pieces,
        preferred_element_type=jnp.float32,
    )
    bias_block = bias.reshape(n_y, n_x, width)
    bias_block = lax.dynamic_index_in_dim(bias_block, lax.axis_index("x"), 1, keepdims=False)
    block_out = (summed + bias_block[None]).astype(jnp.bfloat16)
    swapped = lax.all_to_all(block_out, "x", split_axis=0, concat_axis=1, tiled=True)
    swapped = swapped.reshape(rows, n_x, n_y, width)
    return jnp.transpose(swapped, (0, 2, 1, 3)).reshape(rows, n_y * n_x * width)


def on_device(hidden_in, lengths, attn_norm, qkv_weight, qkv_bias):
    rows = hidden_in.shape[0]
    gy_index = lax.axis_index("y") * lax.axis_size("x") + lax.axis_index("x")
    first = gy_index * rows
    row_lengths = lengths[0]
    qdim = HEADS * HEAD_DIM
    kdim = KV_HEADS * HEAD_DIM
    group = HEADS // KV_HEADS
    normed = norm_rows(hidden_in, attn_norm)
    joined = project_joined(normed, qkv_weight, qkv_bias)
    ends = jnp.cumsum(row_lengths)
    tokens_here = first + jnp.arange(rows, dtype=jnp.int32)
    before = ends[None, :] <= tokens_here[:, None]
    seg_here = jnp.sum(before.astype(jnp.int32), axis=1)
    begin = jnp.sum(jnp.where(before, row_lengths[None, :], 0), axis=1)
    pos = tokens_here - begin
    queries = rotate(joined[:, :qdim], pos, HEADS).reshape(rows, KV_HEADS, group, HEAD_DIM)
    keys = rotate(joined[:, qdim : qdim + kdim], pos, KV_HEADS)
    kv_rows = jnp.concatenate([keys, joined[:, qdim + kdim :]], axis=1)
    piece = lax.all_gather(kv_rows, ("y", "x"), axis=0, tiled=True)
    lead = jnp.max(jnp.where(ends <= first, ends, 0))
    meta = jnp.concatenate(
        [ends, jnp.stack([gy_index, lead // BLOCK, 0, 0]).astype(jnp.int32)]
    ).astype(jnp.int32)
    steps = min(piece.shape[0] // BLOCK, 9)
    queries_t = jnp.transpose(queries.reshape(rows, qdim))
    values_t = jnp.transpose(piece[:, kdim:])
    attn = jnp.transpose(flash(meta, queries_t, piece[:, :kdim], values_t, steps))
    return (attn, kv_rows)


def solution(mesh):
    n_z = len({d.coords[2] for d in mesh.devices.flat})
    grid = mesh.devices.reshape(n_z, -1, *mesh.devices.shape[1:])
    n_y = len({d.coords[1] for d in mesh.devices.flat})
    grid = grid.reshape(grid.shape[0], grid.shape[1], n_y, -1)
    split = jax.sharding.Mesh(grid, ("z", "c", "y", "x"))
    tokens = P(("z", "c", "y", "x"), None)
    placed = (tokens, P(("z", "c"), None), P(), P(("z", "c"), ("y", "x")), P())
    return jax.shard_map(
        on_device,
        mesh=split,
        in_specs=placed,
        out_specs=(tokens, tokens),
        check_vma=False,
    )
```

```python
import math

import jax
import jax.numpy as jnp
from jax import lax
from jax.sharding import PartitionSpec as P
from jax.experimental import pallas as pl
from jax.experimental.pallas import tpu as pltpu

HEADS = 28
KV_HEADS = 4
HEAD_DIM = 128


BLOCK = 256


LANES = 128


def flash_body(meta, q_ref, k_ref, v_ref, o_ref, bias_ref, m_ref, l_ref, acc_ref):
    step = pl.program_id(1)
    last = pl.num_programs(1) - 1
    first = meta[4] * BLOCK
    block = jnp.minimum(meta[5] + step, meta[4])
    group = HEADS // KV_HEADS

    @pl.when(step == 0)
    def _():
        m_ref[...] = jnp.full(m_ref.shape, -1e30, jnp.float32)
        l_ref[...] = jnp.zeros(l_ref.shape, jnp.float32)
        acc_ref[...] = jnp.zeros(acc_ref.shape, jnp.float32)

    @pl.when(meta[5] + step <= meta[4])
    def _():
        krow = block * BLOCK + lax.broadcasted_iota(jnp.int32, (BLOCK, 1), 0)
        qcol = first + lax.broadcasted_iota(jnp.int32, (1, BLOCK), 1)
        qstart = jnp.zeros((1, BLOCK), jnp.int32)
        for s in range(4):
            end = meta[s]
            qstart = jnp.where(end <= qcol, end, qstart)
        allowed = (krow >= qstart) & (krow <= qcol)
        bias_ref[...] = jnp.where(allowed, 0.0, -1e30).astype(jnp.float32)
        keys = k_ref[...]
        values = v_ref[...]
        scale = 1.0 / HEAD_DIM**0.5
        for h in range(group):
            heads = slice(h * HEAD_DIM, (h + 1) * HEAD_DIM)
            for c in range(BLOCK // LANES):
                cols = slice(c * LANES, (c + 1) * LANES)
                q = q_ref[heads, cols]
                scores = (
                    jnp.dot(keys, q, preferred_element_type=jnp.float32) * scale
                    + bias_ref[:, cols]
                )
                m_prev = m_ref[h, :, cols]
                m_new = jnp.maximum(m_prev, jnp.max(scores, axis=0, keepdims=True))
                shrink = jnp.exp(m_prev - m_new)
                weights = jnp.exp(scores - m_new)
                l_ref[h, :, cols] = l_ref[h, :, cols] * shrink + jnp.sum(
                    weights, axis=0, keepdims=True
                )
                acc_ref[h, :, cols] = acc_ref[h, :, cols] * shrink + jnp.dot(
                    values, weights.astype(jnp.bfloat16), preferred_element_type=jnp.float32
                )
                m_ref[h, :, cols] = m_new

    @pl.when(step == last)
    def _():
        for h in range(group):
            o_ref[h * HEAD_DIM : (h + 1) * HEAD_DIM, :] = (acc_ref[h] / l_ref[h]).astype(
                o_ref.dtype
            )


def flash(meta, queries_t, keys, values_t, steps):
    rows = queries_t.shape[1]
    group = HEADS // KV_HEADS
    width = group * HEAD_DIM

    def key_map(g, t, meta):
        return (jnp.minimum(meta[5] + t, meta[4]), g)

    def value_map(g, t, meta):
        return (g, jnp.minimum(meta[5] + t, meta[4]))

    spec = pltpu.PrefetchScalarGridSpec(
        num_scalar_prefetch=1,
        grid=(KV_HEADS, steps),
        in_specs=[
            pl.BlockSpec((width, rows), lambda g, t, meta: (g, 0)),
            pl.BlockSpec((BLOCK, HEAD_DIM), key_map),
            pl.BlockSpec((HEAD_DIM, BLOCK), value_map),
        ],
        out_specs=pl.BlockSpec((width, rows), lambda g, t, meta: (g, 0)),
        scratch_shapes=[
            pltpu.VMEM((BLOCK, rows), jnp.float32),
            pltpu.VMEM((group, 1, rows), jnp.float32),
            pltpu.VMEM((group, 1, rows), jnp.float32),
            pltpu.VMEM((group, HEAD_DIM, rows), jnp.float32),
        ],
    )
    return pl.pallas_call(
        flash_body,
        grid_spec=spec,
        out_shape=jax.ShapeDtypeStruct((HEADS * HEAD_DIM, rows), jnp.bfloat16),
        compiler_params=pltpu.CompilerParams(dimension_semantics=("arbitrary", "arbitrary")),
    )(meta, queries_t, keys, values_t)


def norm_rows(values, gain):
    wide = values.astype(jnp.float32)
    scale = lax.rsqrt(jnp.mean(wide * wide, axis=1, keepdims=True) + 1e-06)
    return (wide * scale * gain[None, :]).astype(jnp.bfloat16)


def segment_of(index, ends):
    return jnp.sum((ends[None, :] <= index[:, None]).astype(jnp.int32), axis=1)


def rotate(block, pos, heads):
    half = HEAD_DIM // 2
    freqs = 1000000.0 ** (-2.0 * jnp.arange(half, dtype=jnp.float32) / HEAD_DIM)
    angle = pos.astype(jnp.float32)[:, None, None] * freqs[None, None, :]
    wide = block.astype(jnp.float32).reshape(block.shape[0], heads, HEAD_DIM)
    first, second = (wide[..., :half], wide[..., half:])
    turned = jnp.concatenate(
        [
            first * jnp.cos(angle) - second * jnp.sin(angle),
            second * jnp.cos(angle) + first * jnp.sin(angle),
        ],
        axis=2,
    )
    return turned.reshape(block.shape[0], heads * HEAD_DIM).astype(jnp.bfloat16)


def project_joined(normed, weight, bias):
    rows, width = normed.shape[0], weight.shape[1]
    n_x = lax.axis_size("x")
    n_y = lax.axis_size("y")
    here = lax.axis_index("x")
    shifted = [normed]
    for step in range(1, n_x):
        pairs = [(s, (s + step) % n_x) for s in range(n_x)]
        shifted.append(lax.ppermute(normed, "x", pairs))
    grouped = jnp.zeros((n_x * rows, normed.shape[1]), normed.dtype)
    for step, piece in enumerate(shifted):
        at = ((here - step) % n_x) * rows
        grouped = lax.dynamic_update_slice_in_dim(grouped, piece, at, 0)
    pieces = lax.all_gather(weight, ("z", "c", "y"), axis=0, tiled=False)
    pieces = pieces.reshape(-1, n_y, weight.shape[0], width)
    summed = jnp.einsum(
        "tie,iyec->tyc",
        grouped.reshape(grouped.shape[0], pieces.shape[0], weight.shape[0]),
        pieces,
        preferred_element_type=jnp.float32,
    )
    bias_block = bias.reshape(n_y, n_x, width)
    bias_block = lax.dynamic_index_in_dim(bias_block, lax.axis_index("x"), 1, keepdims=False)
    block_out = (summed + bias_block[None]).astype(jnp.bfloat16)
    tail = lax.all_to_all(block_out[:, n_y - 1], "x", split_axis=0, concat_axis=1, tiled=True)
    head = block_out[:, : n_y - 1].reshape(block_out.shape[0], -1)
    head = lax.all_to_all(head, "x", split_axis=0, concat_axis=1, tiled=True)
    head = jnp.transpose(head.reshape(rows, n_x, n_y - 1, width), (0, 2, 1, 3))
    return head.reshape(rows, -1), tail


def on_device(hidden_in, lengths, attn_norm, qkv_weight, qkv_bias):
    rows = hidden_in.shape[0]
    gy_index = lax.axis_index("y") * lax.axis_size("x") + lax.axis_index("x")
    first = gy_index * rows
    row_lengths = lengths[0]
    qdim = HEADS * HEAD_DIM
    kdim = KV_HEADS * HEAD_DIM
    group = HEADS // KV_HEADS
    normed = norm_rows(hidden_in, attn_norm)
    head, tail = project_joined(normed, qkv_weight, qkv_bias)
    split = qdim - head.shape[1]
    ends = jnp.cumsum(row_lengths)
    tokens_here = first + jnp.arange(rows, dtype=jnp.int32)
    before = ends[None, :] <= tokens_here[:, None]
    seg_here = jnp.sum(before.astype(jnp.int32), axis=1)
    begin = jnp.sum(jnp.where(before, row_lengths[None, :], 0), axis=1)
    pos = tokens_here - begin
    keys = rotate(tail[:, split : split + kdim], pos, KV_HEADS)
    kv_rows = jnp.concatenate([keys, tail[:, split + kdim :]], axis=1)
    queries = rotate(jnp.concatenate([head, tail[:, :split]], axis=1), pos, HEADS)
    piece = lax.all_gather(kv_rows, ("y", "x"), axis=0, tiled=True)
    lead = jnp.max(jnp.where(ends <= first, ends, 0))
    meta = jnp.concatenate(
        [ends, jnp.stack([gy_index, lead // BLOCK, 0, 0]).astype(jnp.int32)]
    ).astype(jnp.int32)
    steps = min(piece.shape[0] // BLOCK, 9)
    queries_t = jnp.transpose(queries.reshape(rows, qdim))
    values_t = jnp.transpose(piece[:, kdim:])
    attn = jnp.transpose(flash(meta, queries_t, piece[:, :kdim], values_t, steps))
    return (attn, kv_rows)


def solution(mesh):
    n_z = len({d.coords[2] for d in mesh.devices.flat})
    grid = mesh.devices.reshape(n_z, -1, *mesh.devices.shape[1:])
    n_y = len({d.coords[1] for d in mesh.devices.flat})
    grid = grid.reshape(grid.shape[0], grid.shape[1], n_y, -1)
    split = jax.sharding.Mesh(grid, ("z", "c", "y", "x"))
    tokens = P(("z", "c", "y", "x"), None)
    placed = (tokens, P(("z", "c"), None), P(), P(("z", "c"), ("y", "x")), P())
    return jax.shard_map(
        on_device,
        mesh=split,
        in_specs=placed,
        out_specs=(tokens, tokens),
        check_vma=False,
    )
```

```python
import math

import jax
import jax.numpy as jnp
from jax import lax
from jax.sharding import PartitionSpec as P
from jax.experimental import pallas as pl
from jax.experimental.pallas import tpu as pltpu

HEADS = 28
KV_HEADS = 4
HEAD_DIM = 128


BLOCK = 256


LANES = 128


def flash_body(meta, q_ref, k_ref, v_ref, o_ref, bias_ref, m_ref, l_ref, acc_ref):
    step = pl.program_id(1)
    last = pl.num_programs(1) - 1
    first = meta[4] * BLOCK
    block = jnp.minimum(meta[5] + step, meta[4])
    group = HEADS // KV_HEADS

    @pl.when(step == 0)
    def _():
        m_ref[...] = jnp.full(m_ref.shape, -1e30, jnp.float32)
        l_ref[...] = jnp.zeros(l_ref.shape, jnp.float32)
        acc_ref[...] = jnp.zeros(acc_ref.shape, jnp.float32)

    @pl.when(meta[5] + step <= meta[4])
    def _():
        krow = block * BLOCK + lax.broadcasted_iota(jnp.int32, (BLOCK, 1), 0)
        qcol = first + lax.broadcasted_iota(jnp.int32, (1, BLOCK), 1)
        qstart = jnp.zeros((1, BLOCK), jnp.int32)
        for s in range(4):
            end = meta[s]
            qstart = jnp.where(end <= qcol, end, qstart)
        allowed = (krow >= qstart) & (krow <= qcol)
        bias_ref[...] = jnp.where(allowed, 0.0, -1e30).astype(jnp.float32)
        keys = k_ref[...]
        values = jnp.transpose(v_ref[...].astype(jnp.float32)).astype(jnp.bfloat16)
        scale = 1.0 / HEAD_DIM**0.5
        for h in range(group):
            heads = slice(h * HEAD_DIM, (h + 1) * HEAD_DIM)
            for c in range(BLOCK // LANES):
                cols = slice(c * LANES, (c + 1) * LANES)
                q = q_ref[cols, heads]
                scores = (
                    lax.dot_general(
                        keys, q, (((1,), (1,)), ((), ())), preferred_element_type=jnp.float32
                    )
                    * scale
                    + bias_ref[:, cols]
                )
                m_prev = m_ref[h, :, cols]
                m_new = jnp.maximum(m_prev, jnp.max(scores, axis=0, keepdims=True))
                shrink = jnp.exp(m_prev - m_new)
                weights = jnp.exp(scores - m_new)
                l_ref[h, :, cols] = l_ref[h, :, cols] * shrink + jnp.sum(
                    weights, axis=0, keepdims=True
                )
                acc_ref[h, :, cols] = acc_ref[h, :, cols] * shrink + jnp.dot(
                    values, weights.astype(jnp.bfloat16), preferred_element_type=jnp.float32
                )
                m_ref[h, :, cols] = m_new

    @pl.when(step == last)
    def _():
        for h in range(group):
            o_ref[:, h * HEAD_DIM : (h + 1) * HEAD_DIM] = jnp.transpose(
                acc_ref[h] / l_ref[h]
            ).astype(o_ref.dtype)


def flash(meta, queries, kv_all, steps):
    rows = queries.shape[0]
    group = HEADS // KV_HEADS
    width = group * HEAD_DIM

    def key_map(g, t, meta):
        return (jnp.minimum(meta[5] + t, meta[4]), g)

    def value_map(g, t, meta):
        return (jnp.minimum(meta[5] + t, meta[4]), KV_HEADS + g)

    spec = pltpu.PrefetchScalarGridSpec(
        num_scalar_prefetch=1,
        grid=(KV_HEADS, steps),
        in_specs=[
            pl.BlockSpec((rows, width), lambda g, t, meta: (0, g)),
            pl.BlockSpec((BLOCK, HEAD_DIM), key_map),
            pl.BlockSpec((BLOCK, HEAD_DIM), value_map),
        ],
        out_specs=pl.BlockSpec((rows, width), lambda g, t, meta: (0, g)),
        scratch_shapes=[
            pltpu.VMEM((BLOCK, rows), jnp.float32),
            pltpu.VMEM((group, 1, rows), jnp.float32),
            pltpu.VMEM((group, 1, rows), jnp.float32),
            pltpu.VMEM((group, HEAD_DIM, rows), jnp.float32),
        ],
    )
    return pl.pallas_call(
        flash_body,
        grid_spec=spec,
        out_shape=jax.ShapeDtypeStruct((rows, HEADS * HEAD_DIM), jnp.bfloat16),
        compiler_params=pltpu.CompilerParams(dimension_semantics=("arbitrary", "arbitrary")),
    )(meta, queries, kv_all, kv_all)


def norm_rows(values, gain):
    wide = values.astype(jnp.float32)
    scale = lax.rsqrt(jnp.mean(wide * wide, axis=1, keepdims=True) + 1e-06)
    return (wide * scale * gain[None, :]).astype(jnp.bfloat16)


def segment_of(index, ends):
    return jnp.sum((ends[None, :] <= index[:, None]).astype(jnp.int32), axis=1)


def rotate(block, pos, heads):
    half = HEAD_DIM // 2
    freqs = 1000000.0 ** (-2.0 * jnp.arange(half, dtype=jnp.float32) / HEAD_DIM)
    angle = pos.astype(jnp.float32)[:, None, None] * freqs[None, None, :]
    wide = block.astype(jnp.float32).reshape(block.shape[0], heads, HEAD_DIM)
    first, second = (wide[..., :half], wide[..., half:])
    turned = jnp.concatenate(
        [
            first * jnp.cos(angle) - second * jnp.sin(angle),
            second * jnp.cos(angle) + first * jnp.sin(angle),
        ],
        axis=2,
    )
    return turned.reshape(block.shape[0], heads * HEAD_DIM).astype(jnp.bfloat16)


def project_joined(normed, weight, bias):
    rows, width = normed.shape[0], weight.shape[1]
    n_x = lax.axis_size("x")
    n_y = lax.axis_size("y")
    here = lax.axis_index("x")
    shifted = [normed]
    for step in range(1, n_x):
        pairs = [(s, (s + step) % n_x) for s in range(n_x)]
        shifted.append(lax.ppermute(normed, "x", pairs))
    grouped = jnp.zeros((n_x * rows, normed.shape[1]), normed.dtype)
    for step, piece in enumerate(shifted):
        at = ((here - step) % n_x) * rows
        grouped = lax.dynamic_update_slice_in_dim(grouped, piece, at, 0)
    pieces = lax.all_gather(weight, ("z", "c", "y"), axis=0, tiled=False)
    pieces = pieces.reshape(-1, n_y, weight.shape[0], width)
    summed = jnp.einsum(
        "tie,iyec->tyc",
        grouped.reshape(grouped.shape[0], pieces.shape[0], weight.shape[0]),
        pieces,
        preferred_element_type=jnp.float32,
    )
    bias_block = bias.reshape(n_y, n_x, width)
    bias_block = lax.dynamic_index_in_dim(bias_block, lax.axis_index("x"), 1, keepdims=False)
    block_out = (summed + bias_block[None]).astype(jnp.bfloat16)
    tail = lax.all_to_all(block_out[:, n_y - 1], "x", split_axis=0, concat_axis=1, tiled=True)
    head = block_out[:, : n_y - 1].reshape(block_out.shape[0], -1)
    head = lax.all_to_all(head, "x", split_axis=0, concat_axis=1, tiled=True)
    head = jnp.transpose(head.reshape(rows, n_x, n_y - 1, width), (0, 2, 1, 3))
    return head.reshape(rows, -1), tail


def on_device(hidden_in, lengths, attn_norm, qkv_weight, qkv_bias):
    rows = hidden_in.shape[0]
    gy_index = lax.axis_index("y") * lax.axis_size("x") + lax.axis_index("x")
    first = gy_index * rows
    row_lengths = lengths[0]
    qdim = HEADS * HEAD_DIM
    kdim = KV_HEADS * HEAD_DIM
    group = HEADS // KV_HEADS
    normed = norm_rows(hidden_in, attn_norm)
    head, tail = project_joined(normed, qkv_weight, qkv_bias)
    split = qdim - head.shape[1]
    ends = jnp.cumsum(row_lengths)
    tokens_here = first + jnp.arange(rows, dtype=jnp.int32)
    before = ends[None, :] <= tokens_here[:, None]
    seg_here = jnp.sum(before.astype(jnp.int32), axis=1)
    begin = jnp.sum(jnp.where(before, row_lengths[None, :], 0), axis=1)
    pos = tokens_here - begin
    keys = rotate(tail[:, split : split + kdim], pos, KV_HEADS)
    kv_rows = jnp.concatenate([keys, tail[:, split + kdim :]], axis=1)
    queries = rotate(jnp.concatenate([head, tail[:, :split]], axis=1), pos, HEADS)
    piece = lax.all_gather(kv_rows, ("y", "x"), axis=0, tiled=True)
    lead = jnp.max(jnp.where(ends <= first, ends, 0))
    meta = jnp.concatenate(
        [ends, jnp.stack([gy_index, lead // BLOCK, 0, 0]).astype(jnp.int32)]
    ).astype(jnp.int32)
    steps = min(piece.shape[0] // BLOCK, 9)
    attn = flash(meta, queries, piece, steps)
    return (attn, kv_rows)


def solution(mesh):
    n_z = len({d.coords[2] for d in mesh.devices.flat})
    grid = mesh.devices.reshape(n_z, -1, *mesh.devices.shape[1:])
    n_y = len({d.coords[1] for d in mesh.devices.flat})
    grid = grid.reshape(grid.shape[0], grid.shape[1], n_y, -1)
    split = jax.sharding.Mesh(grid, ("z", "c", "y", "x"))
    tokens = P(("z", "c", "y", "x"), None)
    placed = (tokens, P(("z", "c"), None), P(), P(("z", "c"), ("y", "x")), P())
    return jax.shard_map(
        on_device,
        mesh=split,
        in_specs=placed,
        out_specs=(tokens, tokens),
        check_vma=False,
    )
```

```python
import math

import jax
import jax.numpy as jnp
from jax import lax
from jax.sharding import PartitionSpec as P
from jax.experimental import pallas as pl
from jax.experimental.pallas import tpu as pltpu

HEADS = 28
KV_HEADS = 4
HEAD_DIM = 128


BLOCK = 256


LANES = 128


def flash_body(meta, q_ref, k_ref, v_ref, o_ref, bias_ref, m_ref, l_ref, acc_ref):
    step = pl.program_id(1)
    last = pl.num_programs(1) - 1
    first = meta[4] * BLOCK
    block = jnp.minimum(meta[5] + step, meta[4])
    group = HEADS // KV_HEADS

    @pl.when(step == 0)
    def _():
        m_ref[...] = jnp.full(m_ref.shape, -1e30, jnp.float32)
        l_ref[...] = jnp.zeros(l_ref.shape, jnp.float32)
        acc_ref[...] = jnp.zeros(acc_ref.shape, jnp.float32)

    @pl.when(meta[5] + step <= meta[4])
    def _():
        krow = block * BLOCK + lax.broadcasted_iota(jnp.int32, (BLOCK, 1), 0)
        qcol = first + lax.broadcasted_iota(jnp.int32, (1, BLOCK), 1)
        qstart = jnp.zeros((1, BLOCK), jnp.int32)
        for s in range(4):
            end = meta[s]
            qstart = jnp.where(end <= qcol, end, qstart)
        allowed = (krow >= qstart) & (krow <= qcol)
        bias_ref[...] = jnp.where(allowed, 0.0, -1e30).astype(jnp.float32)
        keys = k_ref[...]
        values = jnp.transpose(v_ref[...].astype(jnp.float32)).astype(jnp.bfloat16)
        scale = 1.0 / HEAD_DIM**0.5
        for h in range(group):
            heads = slice(h * HEAD_DIM, (h + 1) * HEAD_DIM)
            for c in range(BLOCK // LANES):
                cols = slice(c * LANES, (c + 1) * LANES)
                q = q_ref[heads, cols]
                scores = (
                    jnp.dot(keys, q, preferred_element_type=jnp.float32) * scale
                    + bias_ref[:, cols]
                )
                m_prev = m_ref[h, :, cols]
                m_new = jnp.maximum(m_prev, jnp.max(scores, axis=0, keepdims=True))
                shrink = jnp.exp(m_prev - m_new)
                weights = jnp.exp(scores - m_new)
                l_ref[h, :, cols] = l_ref[h, :, cols] * shrink + jnp.sum(
                    weights, axis=0, keepdims=True
                )
                acc_ref[h, :, cols] = acc_ref[h, :, cols] * shrink + jnp.dot(
                    values, weights.astype(jnp.bfloat16), preferred_element_type=jnp.float32
                )
                m_ref[h, :, cols] = m_new

    @pl.when(step == last)
    def _():
        for h in range(group):
            o_ref[:, h * HEAD_DIM : (h + 1) * HEAD_DIM] = jnp.transpose(
                acc_ref[h] / l_ref[h]
            ).astype(o_ref.dtype)


def flash(meta, queries_t, kv_all, steps):
    rows = queries_t.shape[1]
    group = HEADS // KV_HEADS
    width = group * HEAD_DIM

    def key_map(g, t, meta):
        return (jnp.minimum(meta[5] + t, meta[4]), g)

    def value_map(g, t, meta):
        return (jnp.minimum(meta[5] + t, meta[4]), KV_HEADS + g)

    spec = pltpu.PrefetchScalarGridSpec(
        num_scalar_prefetch=1,
        grid=(KV_HEADS, steps),
        in_specs=[
            pl.BlockSpec((width, rows), lambda g, t, meta: (g, 0)),
            pl.BlockSpec((BLOCK, HEAD_DIM), key_map),
            pl.BlockSpec((BLOCK, HEAD_DIM), value_map),
        ],
        out_specs=pl.BlockSpec((rows, width), lambda g, t, meta: (0, g)),
        scratch_shapes=[
            pltpu.VMEM((BLOCK, rows), jnp.float32),
            pltpu.VMEM((group, 1, rows), jnp.float32),
            pltpu.VMEM((group, 1, rows), jnp.float32),
            pltpu.VMEM((group, HEAD_DIM, rows), jnp.float32),
        ],
    )
    return pl.pallas_call(
        flash_body,
        grid_spec=spec,
        out_shape=jax.ShapeDtypeStruct((rows, HEADS * HEAD_DIM), jnp.bfloat16),
        compiler_params=pltpu.CompilerParams(dimension_semantics=("arbitrary", "arbitrary")),
    )(meta, queries_t, kv_all, kv_all)


def norm_rows(values, gain):
    wide = values.astype(jnp.float32)
    scale = lax.rsqrt(jnp.mean(wide * wide, axis=1, keepdims=True) + 1e-06)
    return (wide * scale * gain[None, :]).astype(jnp.bfloat16)


def segment_of(index, ends):
    return jnp.sum((ends[None, :] <= index[:, None]).astype(jnp.int32), axis=1)


def rotate(block, pos, heads):
    half = HEAD_DIM // 2
    freqs = 1000000.0 ** (-2.0 * jnp.arange(half, dtype=jnp.float32) / HEAD_DIM)
    angle = pos.astype(jnp.float32)[:, None, None] * freqs[None, None, :]
    wide = block.astype(jnp.float32).reshape(block.shape[0], heads, HEAD_DIM)
    first, second = (wide[..., :half], wide[..., half:])
    turned = jnp.concatenate(
        [
            first * jnp.cos(angle) - second * jnp.sin(angle),
            second * jnp.cos(angle) + first * jnp.sin(angle),
        ],
        axis=2,
    )
    return turned.reshape(block.shape[0], heads * HEAD_DIM).astype(jnp.bfloat16)


def project_joined(normed, weight, bias):
    rows, width = normed.shape[0], weight.shape[1]
    n_x = lax.axis_size("x")
    n_y = lax.axis_size("y")
    here = lax.axis_index("x")
    shifted = [normed]
    for step in range(1, n_x):
        pairs = [(s, (s + step) % n_x) for s in range(n_x)]
        shifted.append(lax.ppermute(normed, "x", pairs))
    grouped = jnp.zeros((n_x * rows, normed.shape[1]), normed.dtype)
    for step, piece in enumerate(shifted):
        at = ((here - step) % n_x) * rows
        grouped = lax.dynamic_update_slice_in_dim(grouped, piece, at, 0)
    pieces = lax.all_gather(weight, ("z", "c", "y"), axis=0, tiled=False)
    pieces = pieces.reshape(-1, n_y, weight.shape[0], width)
    summed = jnp.einsum(
        "tie,iyec->tyc",
        grouped.reshape(grouped.shape[0], pieces.shape[0], weight.shape[0]),
        pieces,
        preferred_element_type=jnp.float32,
    )
    bias_block = bias.reshape(n_y, n_x, width)
    bias_block = lax.dynamic_index_in_dim(bias_block, lax.axis_index("x"), 1, keepdims=False)
    block_out = (summed + bias_block[None]).astype(jnp.bfloat16)
    tail = lax.all_to_all(block_out[:, n_y - 1], "x", split_axis=0, concat_axis=1, tiled=True)
    head = block_out[:, : n_y - 1].reshape(block_out.shape[0], -1)
    head = lax.all_to_all(head, "x", split_axis=0, concat_axis=1, tiled=True)
    head = jnp.transpose(head.reshape(rows, n_x, n_y - 1, width), (0, 2, 1, 3))
    return head.reshape(rows, -1), tail


def on_device(hidden_in, lengths, attn_norm, qkv_weight, qkv_bias):
    rows = hidden_in.shape[0]
    gy_index = lax.axis_index("y") * lax.axis_size("x") + lax.axis_index("x")
    first = gy_index * rows
    row_lengths = lengths[0]
    qdim = HEADS * HEAD_DIM
    kdim = KV_HEADS * HEAD_DIM
    group = HEADS // KV_HEADS
    normed = norm_rows(hidden_in, attn_norm)
    head, tail = project_joined(normed, qkv_weight, qkv_bias)
    split = qdim - head.shape[1]
    ends = jnp.cumsum(row_lengths)
    tokens_here = first + jnp.arange(rows, dtype=jnp.int32)
    before = ends[None, :] <= tokens_here[:, None]
    seg_here = jnp.sum(before.astype(jnp.int32), axis=1)
    begin = jnp.sum(jnp.where(before, row_lengths[None, :], 0), axis=1)
    pos = tokens_here - begin
    keys = rotate(tail[:, split : split + kdim], pos, KV_HEADS)
    kv_rows = jnp.concatenate([keys, tail[:, split + kdim :]], axis=1)
    queries = rotate(jnp.concatenate([head, tail[:, :split]], axis=1), pos, HEADS)
    piece = lax.all_gather(kv_rows, ("y", "x"), axis=0, tiled=True)
    lead = jnp.max(jnp.where(ends <= first, ends, 0))
    meta = jnp.concatenate(
        [ends, jnp.stack([gy_index, lead // BLOCK, 0, 0]).astype(jnp.int32)]
    ).astype(jnp.int32)
    steps = min(piece.shape[0] // BLOCK, 9)
    attn = flash(meta, jnp.transpose(queries), piece, steps)
    return (attn, kv_rows)


def solution(mesh):
    n_z = len({d.coords[2] for d in mesh.devices.flat})
    grid = mesh.devices.reshape(n_z, -1, *mesh.devices.shape[1:])
    n_y = len({d.coords[1] for d in mesh.devices.flat})
    grid = grid.reshape(grid.shape[0], grid.shape[1], n_y, -1)
    split = jax.sharding.Mesh(grid, ("z", "c", "y", "x"))
    tokens = P(("z", "c", "y", "x"), None)
    placed = (tokens, P(("z", "c"), None), P(), P(("z", "c"), ("y", "x")), P())
    return jax.shard_map(
        on_device,
        mesh=split,
        in_specs=placed,
        out_specs=(tokens, tokens),
        check_vma=False,
    )
```

```python
import math

import jax
import jax.numpy as jnp
from jax import lax
from jax.sharding import PartitionSpec as P
from jax.experimental import pallas as pl
from jax.experimental.pallas import tpu as pltpu

HEADS = 28
KV_HEADS = 4
HEAD_DIM = 128


BLOCK = 256


LANES = 128


def flash_body(meta, q_ref, k_ref, v_ref, o_ref, bias_ref, m_ref, l_ref, acc_ref):
    step = pl.program_id(1)
    last = pl.num_programs(1) - 1
    first = meta[4] * BLOCK
    block = jnp.minimum(meta[5] + step, meta[4])
    group = HEADS // KV_HEADS

    @pl.when(step == 0)
    def _():
        m_ref[...] = jnp.full(m_ref.shape, -1e30, jnp.float32)
        l_ref[...] = jnp.zeros(l_ref.shape, jnp.float32)
        acc_ref[...] = jnp.zeros(acc_ref.shape, jnp.float32)

    @pl.when(meta[5] + step <= meta[4])
    def _():
        krow = block * BLOCK + lax.broadcasted_iota(jnp.int32, (BLOCK, 1), 0)
        qcol = first + lax.broadcasted_iota(jnp.int32, (1, BLOCK), 1)
        qstart = jnp.zeros((1, BLOCK), jnp.int32)
        for s in range(4):
            end = meta[s]
            qstart = jnp.where(end <= qcol, end, qstart)
        allowed = (krow >= qstart) & (krow <= qcol)
        bias_ref[...] = jnp.where(allowed, 0.0, -1e30).astype(jnp.float32)
        keys = k_ref[...]
        values = jnp.transpose(v_ref[...].astype(jnp.float32)).astype(jnp.bfloat16)
        scale = 1.0 / HEAD_DIM**0.5
        for h in range(group):
            heads = slice(h * HEAD_DIM, (h + 1) * HEAD_DIM)
            for c in range(BLOCK // LANES):
                cols = slice(c * LANES, (c + 1) * LANES)
                q = q_ref[heads, cols]
                scores = (
                    jnp.dot(keys, q, preferred_element_type=jnp.float32) * scale
                    + bias_ref[:, cols]
                )
                m_prev = m_ref[h, :, cols]
                m_new = jnp.maximum(m_prev, jnp.max(scores, axis=0, keepdims=True))
                shrink = jnp.exp(m_prev - m_new)
                weights = jnp.exp(scores - m_new)
                l_ref[h, :, cols] = l_ref[h, :, cols] * shrink + jnp.sum(
                    weights, axis=0, keepdims=True
                )
                acc_ref[h, :, cols] = acc_ref[h, :, cols] * shrink + jnp.dot(
                    values, weights.astype(jnp.bfloat16), preferred_element_type=jnp.float32
                )
                m_ref[h, :, cols] = m_new

    @pl.when(step == last)
    def _():
        for h in range(group):
            o_ref[:, h * HEAD_DIM : (h + 1) * HEAD_DIM] = jnp.transpose(
                acc_ref[h] / l_ref[h]
            ).astype(o_ref.dtype)


def flash(meta, queries_t, kv_all, steps):
    rows = queries_t.shape[1]
    group = HEADS // KV_HEADS
    width = group * HEAD_DIM

    def key_map(g, t, meta):
        return (jnp.minimum(meta[5] + t, meta[4]), g)

    def value_map(g, t, meta):
        return (jnp.minimum(meta[5] + t, meta[4]), KV_HEADS + g)

    spec = pltpu.PrefetchScalarGridSpec(
        num_scalar_prefetch=1,
        grid=(KV_HEADS, steps),
        in_specs=[
            pl.BlockSpec((width, rows), lambda g, t, meta: (g, 0)),
            pl.BlockSpec((BLOCK, HEAD_DIM), key_map),
            pl.BlockSpec((BLOCK, HEAD_DIM), value_map),
        ],
        out_specs=pl.BlockSpec((rows, width), lambda g, t, meta: (0, g)),
        scratch_shapes=[
            pltpu.VMEM((BLOCK, rows), jnp.float32),
            pltpu.VMEM((group, 1, rows), jnp.float32),
            pltpu.VMEM((group, 1, rows), jnp.float32),
            pltpu.VMEM((group, HEAD_DIM, rows), jnp.float32),
        ],
    )
    return pl.pallas_call(
        flash_body,
        grid_spec=spec,
        out_shape=jax.ShapeDtypeStruct((rows, HEADS * HEAD_DIM), jnp.bfloat16),
        compiler_params=pltpu.CompilerParams(dimension_semantics=("arbitrary", "arbitrary")),
    )(meta, queries_t, kv_all, kv_all)


def norm_rows(values, gain):
    wide = values.astype(jnp.float32)
    scale = lax.rsqrt(jnp.mean(wide * wide, axis=1, keepdims=True) + 1e-06)
    return (wide * scale * gain[None, :]).astype(jnp.bfloat16)


def segment_of(index, ends):
    return jnp.sum((ends[None, :] <= index[:, None]).astype(jnp.int32), axis=1)


def rotate(block, pos, heads):
    half = HEAD_DIM // 2
    freqs = 1000000.0 ** (-2.0 * jnp.arange(half, dtype=jnp.float32) / HEAD_DIM)
    angle = pos.astype(jnp.float32)[:, None, None] * freqs[None, None, :]
    wide = block.astype(jnp.float32).reshape(block.shape[0], heads, HEAD_DIM)
    first, second = (wide[..., :half], wide[..., half:])
    turned = jnp.concatenate(
        [
            first * jnp.cos(angle) - second * jnp.sin(angle),
            second * jnp.cos(angle) + first * jnp.sin(angle),
        ],
        axis=2,
    )
    return turned.reshape(block.shape[0], heads * HEAD_DIM).astype(jnp.bfloat16)


def project_joined(normed, weight, bias):
    rows, width = normed.shape[0], weight.shape[1]
    n_x = lax.axis_size("x")
    n_y = lax.axis_size("y")
    here = lax.axis_index("x")
    shifted = [normed]
    for step in range(1, n_x):
        pairs = [(s, (s + step) % n_x) for s in range(n_x)]
        shifted.append(lax.ppermute(normed, "x", pairs))
    grouped = jnp.zeros((n_x * rows, normed.shape[1]), normed.dtype)
    for step, piece in enumerate(shifted):
        at = ((here - step) % n_x) * rows
        grouped = lax.dynamic_update_slice_in_dim(grouped, piece, at, 0)
    pieces = lax.all_gather(weight, ("z", "c", "y"), axis=0, tiled=False)
    pieces = pieces.reshape(-1, n_y, weight.shape[0], width)
    summed = jnp.einsum(
        "tie,iyec->tyc",
        grouped.reshape(grouped.shape[0], pieces.shape[0], weight.shape[0]),
        pieces,
        preferred_element_type=jnp.float32,
    )
    bias_block = bias.reshape(n_y, n_x, width)
    bias_block = lax.dynamic_index_in_dim(bias_block, lax.axis_index("x"), 1, keepdims=False)
    block_out = (summed + bias_block[None]).astype(jnp.bfloat16)

    def exchange(part):
        mine = lax.dynamic_slice_in_dim(part, here * rows, rows, 0)
        full = jnp.zeros((rows, n_x) + part.shape[1:], part.dtype)
        full = lax.dynamic_update_slice_in_dim(full, mine[:, None], here, 1)
        for step in range(1, n_x):
            sent = lax.dynamic_slice_in_dim(part, ((here + step) % n_x) * rows, rows, 0)
            pairs = [(s, (s + step) % n_x) for s in range(n_x)]
            got = lax.ppermute(sent, "x", pairs)
            full = lax.dynamic_update_slice_in_dim(full, got[:, None], (here - step) % n_x, 1)
        return full

    tail = exchange(block_out[:, n_y - 1]).reshape(rows, -1)
    head = exchange(block_out[:, : n_y - 1])
    head = jnp.transpose(head, (0, 2, 1, 3))
    return head.reshape(rows, -1), tail


def on_device(hidden_in, lengths, attn_norm, qkv_weight, qkv_bias):
    rows = hidden_in.shape[0]
    gy_index = lax.axis_index("y") * lax.axis_size("x") + lax.axis_index("x")
    first = gy_index * rows
    row_lengths = lengths[0]
    qdim = HEADS * HEAD_DIM
    kdim = KV_HEADS * HEAD_DIM
    group = HEADS // KV_HEADS
    normed = norm_rows(hidden_in, attn_norm)
    head, tail = project_joined(normed, qkv_weight, qkv_bias)
    split = qdim - head.shape[1]
    ends = jnp.cumsum(row_lengths)
    tokens_here = first + jnp.arange(rows, dtype=jnp.int32)
    before = ends[None, :] <= tokens_here[:, None]
    seg_here = jnp.sum(before.astype(jnp.int32), axis=1)
    begin = jnp.sum(jnp.where(before, row_lengths[None, :], 0), axis=1)
    pos = tokens_here - begin
    keys = rotate(tail[:, split : split + kdim], pos, KV_HEADS)
    kv_rows = jnp.concatenate([keys, tail[:, split + kdim :]], axis=1)
    queries = rotate(jnp.concatenate([head, tail[:, :split]], axis=1), pos, HEADS)
    piece = lax.all_gather(kv_rows, ("y", "x"), axis=0, tiled=True)
    lead = jnp.max(jnp.where(ends <= first, ends, 0))
    meta = jnp.concatenate(
        [ends, jnp.stack([gy_index, lead // BLOCK, 0, 0]).astype(jnp.int32)]
    ).astype(jnp.int32)
    steps = min(piece.shape[0] // BLOCK, 9)
    attn = flash(meta, jnp.transpose(queries), piece, steps)
    return (attn, kv_rows)


def solution(mesh):
    n_z = len({d.coords[2] for d in mesh.devices.flat})
    grid = mesh.devices.reshape(n_z, -1, *mesh.devices.shape[1:])
    n_y = len({d.coords[1] for d in mesh.devices.flat})
    grid = grid.reshape(grid.shape[0], grid.shape[1], n_y, -1)
    split = jax.sharding.Mesh(grid, ("z", "c", "y", "x"))
    tokens = P(("z", "c", "y", "x"), None)
    placed = (tokens, P(("z", "c"), None), P(), P(("z", "c"), ("y", "x")), P())
    return jax.shard_map(
        on_device,
        mesh=split,
        in_specs=placed,
        out_specs=(tokens, tokens),
        check_vma=False,
    )
```

```python
import math

import jax
import jax.numpy as jnp
from jax import lax
from jax.sharding import PartitionSpec as P
from jax.experimental import pallas as pl
from jax.experimental.pallas import tpu as pltpu

HEADS = 28
KV_HEADS = 4
HEAD_DIM = 128


BLOCK = 256


LANES = 128


def flash_body(meta, q_ref, k_ref, v_ref, o_ref, bias_ref, m_ref, l_ref, acc_ref):
    step = pl.program_id(1)
    last = pl.num_programs(1) - 1
    first = meta[4] * BLOCK
    block = jnp.minimum(meta[5] + step, meta[4])
    group = HEADS // KV_HEADS

    @pl.when(step == 0)
    def _():
        m_ref[...] = jnp.full(m_ref.shape, -1e30, jnp.float32)
        l_ref[...] = jnp.zeros(l_ref.shape, jnp.float32)
        acc_ref[...] = jnp.zeros(acc_ref.shape, jnp.float32)

    @pl.when(meta[5] + step <= meta[4])
    def _():
        krow = block * BLOCK + lax.broadcasted_iota(jnp.int32, (BLOCK, 1), 0)
        qcol = first + lax.broadcasted_iota(jnp.int32, (1, BLOCK), 1)
        qstart = jnp.zeros((1, BLOCK), jnp.int32)
        for s in range(4):
            end = meta[s]
            qstart = jnp.where(end <= qcol, end, qstart)
        allowed = (krow >= qstart) & (krow <= qcol)
        bias_ref[...] = jnp.where(allowed, 0.0, -1e30).astype(jnp.float32)
        keys = k_ref[...]
        values = jnp.transpose(v_ref[...].astype(jnp.float32)).astype(jnp.bfloat16)
        scale = 1.0 / HEAD_DIM**0.5
        for h in range(group):
            heads = slice(h * HEAD_DIM, (h + 1) * HEAD_DIM)
            for c in range(BLOCK // LANES):
                cols = slice(c * LANES, (c + 1) * LANES)
                q = q_ref[heads, cols]
                scores = (
                    jnp.dot(keys, q, preferred_element_type=jnp.float32) * scale
                    + bias_ref[:, cols]
                )
                m_prev = m_ref[h, :, cols]
                m_new = jnp.maximum(m_prev, jnp.max(scores, axis=0, keepdims=True))
                shrink = jnp.exp(m_prev - m_new)
                weights = jnp.exp(scores - m_new)
                l_ref[h, :, cols] = l_ref[h, :, cols] * shrink + jnp.sum(
                    weights, axis=0, keepdims=True
                )
                acc_ref[h, :, cols] = acc_ref[h, :, cols] * shrink + jnp.dot(
                    values, weights.astype(jnp.bfloat16), preferred_element_type=jnp.float32
                )
                m_ref[h, :, cols] = m_new

    @pl.when(step == last)
    def _():
        for h in range(group):
            o_ref[:, h * HEAD_DIM : (h + 1) * HEAD_DIM] = jnp.transpose(
                acc_ref[h] / l_ref[h]
            ).astype(o_ref.dtype)


def flash(meta, queries_t, kv_all, steps):
    rows = queries_t.shape[1]
    group = HEADS // KV_HEADS
    width = group * HEAD_DIM

    def key_map(g, t, meta):
        return (jnp.minimum(meta[5] + t, meta[4]), g)

    def value_map(g, t, meta):
        return (jnp.minimum(meta[5] + t, meta[4]), KV_HEADS + g)

    spec = pltpu.PrefetchScalarGridSpec(
        num_scalar_prefetch=1,
        grid=(KV_HEADS, steps),
        in_specs=[
            pl.BlockSpec((width, rows), lambda g, t, meta: (g, 0)),
            pl.BlockSpec((BLOCK, HEAD_DIM), key_map),
            pl.BlockSpec((BLOCK, HEAD_DIM), value_map),
        ],
        out_specs=pl.BlockSpec((rows, width), lambda g, t, meta: (0, g)),
        scratch_shapes=[
            pltpu.VMEM((BLOCK, rows), jnp.float32),
            pltpu.VMEM((group, 1, rows), jnp.float32),
            pltpu.VMEM((group, 1, rows), jnp.float32),
            pltpu.VMEM((group, HEAD_DIM, rows), jnp.float32),
        ],
    )
    return pl.pallas_call(
        flash_body,
        grid_spec=spec,
        out_shape=jax.ShapeDtypeStruct((rows, HEADS * HEAD_DIM), jnp.bfloat16),
        compiler_params=pltpu.CompilerParams(dimension_semantics=("arbitrary", "arbitrary")),
    )(meta, queries_t, kv_all, kv_all)


def norm_rows(values, gain):
    wide = values.astype(jnp.float32)
    scale = lax.rsqrt(jnp.mean(wide * wide, axis=1, keepdims=True) + 1e-06)
    return (wide * scale * gain[None, :]).astype(jnp.bfloat16)


def segment_of(index, ends):
    return jnp.sum((ends[None, :] <= index[:, None]).astype(jnp.int32), axis=1)


def rotate(block, pos, heads):
    half = HEAD_DIM // 2
    freqs = 1000000.0 ** (-2.0 * jnp.arange(half, dtype=jnp.float32) / HEAD_DIM)
    angle = pos.astype(jnp.float32)[:, None, None] * freqs[None, None, :]
    wide = block.astype(jnp.float32).reshape(block.shape[0], heads, HEAD_DIM)
    first, second = (wide[..., :half], wide[..., half:])
    turned = jnp.concatenate(
        [
            first * jnp.cos(angle) - second * jnp.sin(angle),
            second * jnp.cos(angle) + first * jnp.sin(angle),
        ],
        axis=2,
    )
    return turned.reshape(block.shape[0], heads * HEAD_DIM).astype(jnp.bfloat16)


def project_joined(normed, weight, bias):
    rows, width = normed.shape[0], weight.shape[1]
    n_x = lax.axis_size("x")
    n_y = lax.axis_size("y")
    here = lax.axis_index("x")
    shifted = [normed]
    for step in range(1, n_x):
        pairs = [(s, (s + step) % n_x) for s in range(n_x)]
        shifted.append(lax.ppermute(normed, "x", pairs))
    grouped = jnp.zeros((n_x * rows, normed.shape[1]), normed.dtype)
    for step, piece in enumerate(shifted):
        at = ((here - step) % n_x) * rows
        grouped = lax.dynamic_update_slice_in_dim(grouped, piece, at, 0)
    pieces = lax.all_gather(weight, ("z", "c", "y"), axis=0, tiled=False)
    pieces = pieces.reshape(-1, n_y, weight.shape[0], width)
    pieces = jnp.transpose(pieces, (0, 2, 1, 3)).reshape(grouped.shape[1], n_y, width)
    summed = jnp.einsum("td,dyc->tyc", grouped, pieces, preferred_element_type=jnp.float32)
    bias_block = bias.reshape(n_y, n_x, width)
    bias_block = lax.dynamic_index_in_dim(bias_block, lax.axis_index("x"), 1, keepdims=False)
    block_out = (summed + bias_block[None]).astype(jnp.bfloat16)

    def exchange(part):
        mine = lax.dynamic_slice_in_dim(part, here * rows, rows, 0)
        full = jnp.zeros((rows, n_x) + part.shape[1:], part.dtype)
        full = lax.dynamic_update_slice_in_dim(full, mine[:, None], here, 1)
        for step in range(1, n_x):
            sent = lax.dynamic_slice_in_dim(part, ((here + step) % n_x) * rows, rows, 0)
            pairs = [(s, (s + step) % n_x) for s in range(n_x)]
            got = lax.ppermute(sent, "x", pairs)
            full = lax.dynamic_update_slice_in_dim(full, got[:, None], (here - step) % n_x, 1)
        return full

    tail = exchange(block_out[:, n_y - 1]).reshape(rows, -1)
    head = exchange(block_out[:, : n_y - 1])
    head = jnp.transpose(head, (0, 2, 1, 3))
    return head.reshape(rows, -1), tail


def on_device(hidden_in, lengths, attn_norm, qkv_weight, qkv_bias):
    rows = hidden_in.shape[0]
    gy_index = lax.axis_index("y") * lax.axis_size("x") + lax.axis_index("x")
    first = gy_index * rows
    row_lengths = lengths[0]
    qdim = HEADS * HEAD_DIM
    kdim = KV_HEADS * HEAD_DIM
    group = HEADS // KV_HEADS
    normed = norm_rows(hidden_in, attn_norm)
    head, tail = project_joined(normed, qkv_weight, qkv_bias)
    split = qdim - head.shape[1]
    ends = jnp.cumsum(row_lengths)
    tokens_here = first + jnp.arange(rows, dtype=jnp.int32)
    before = ends[None, :] <= tokens_here[:, None]
    seg_here = jnp.sum(before.astype(jnp.int32), axis=1)
    begin = jnp.sum(jnp.where(before, row_lengths[None, :], 0), axis=1)
    pos = tokens_here - begin
    keys = rotate(tail[:, split : split + kdim], pos, KV_HEADS)
    kv_rows = jnp.concatenate([keys, tail[:, split + kdim :]], axis=1)
    queries = rotate(jnp.concatenate([head, tail[:, :split]], axis=1), pos, HEADS)
    piece = lax.all_gather(kv_rows, ("y", "x"), axis=0, tiled=True)
    lead = jnp.max(jnp.where(ends <= first, ends, 0))
    meta = jnp.concatenate(
        [ends, jnp.stack([gy_index, lead // BLOCK, 0, 0]).astype(jnp.int32)]
    ).astype(jnp.int32)
    steps = min(piece.shape[0] // BLOCK, 9)
    attn = flash(meta, jnp.transpose(queries), piece, steps)
    return (attn, kv_rows)


def solution(mesh):
    n_z = len({d.coords[2] for d in mesh.devices.flat})
    grid = mesh.devices.reshape(n_z, -1, *mesh.devices.shape[1:])
    n_y = len({d.coords[1] for d in mesh.devices.flat})
    grid = grid.reshape(grid.shape[0], grid.shape[1], n_y, -1)
    split = jax.sharding.Mesh(grid, ("z", "c", "y", "x"))
    tokens = P(("z", "c", "y", "x"), None)
    placed = (tokens, P(("z", "c"), None), P(), P(("z", "c"), ("y", "x")), P())
    return jax.shard_map(
        on_device,
        mesh=split,
        in_specs=placed,
        out_specs=(tokens, tokens),
        check_vma=False,
    )
```

```python
import math

import jax
import jax.numpy as jnp
from jax import lax
from jax.sharding import PartitionSpec as P
from jax.experimental import pallas as pl
from jax.experimental.pallas import tpu as pltpu

HEADS = 28
KV_HEADS = 4
HEAD_DIM = 128


BLOCK = 256


LANES = 128


def flash_body(meta, q_ref, k_ref, v_ref, o_ref, bias_ref, m_ref, l_ref, acc_ref):
    step = pl.program_id(1)
    last = pl.num_programs(1) - 1
    first = meta[4] * BLOCK
    block = jnp.minimum(meta[5] + step, meta[4])
    group = HEADS // KV_HEADS

    @pl.when(step == 0)
    def _():
        m_ref[...] = jnp.full(m_ref.shape, -1e30, jnp.float32)
        l_ref[...] = jnp.zeros(l_ref.shape, jnp.float32)
        acc_ref[...] = jnp.zeros(acc_ref.shape, jnp.float32)

    @pl.when(meta[5] + step <= meta[4])
    def _():
        krow = block * BLOCK + lax.broadcasted_iota(jnp.int32, (BLOCK, 1), 0)
        qcol = first + lax.broadcasted_iota(jnp.int32, (1, BLOCK), 1)
        qstart = jnp.zeros((1, BLOCK), jnp.int32)
        for s in range(4):
            end = meta[s]
            qstart = jnp.where(end <= qcol, end, qstart)
        allowed = (krow >= qstart) & (krow <= qcol)
        bias_ref[...] = jnp.where(allowed, 0.0, -1e30).astype(jnp.float32)
        keys = k_ref[...]
        values = jnp.transpose(v_ref[...].astype(jnp.float32)).astype(jnp.bfloat16)
        scale = 1.0 / HEAD_DIM**0.5
        for h in range(group):
            heads = slice(h * HEAD_DIM, (h + 1) * HEAD_DIM)
            for c in range(BLOCK // LANES):
                cols = slice(c * LANES, (c + 1) * LANES)
                q = q_ref[heads, cols]
                scores = (
                    jnp.dot(keys, q, preferred_element_type=jnp.float32) * scale
                    + bias_ref[:, cols]
                )
                m_prev = m_ref[h, :, cols]
                m_new = jnp.maximum(m_prev, jnp.max(scores, axis=0, keepdims=True))
                shrink = jnp.exp(m_prev - m_new)
                weights = jnp.exp(scores - m_new)
                l_ref[h, :, cols] = l_ref[h, :, cols] * shrink + jnp.sum(
                    weights, axis=0, keepdims=True
                )
                acc_ref[h, :, cols] = acc_ref[h, :, cols] * shrink + jnp.dot(
                    values, weights.astype(jnp.bfloat16), preferred_element_type=jnp.float32
                )
                m_ref[h, :, cols] = m_new

    @pl.when(step == last)
    def _():
        for h in range(group):
            o_ref[:, h * HEAD_DIM : (h + 1) * HEAD_DIM] = jnp.transpose(
                acc_ref[h] / l_ref[h]
            ).astype(o_ref.dtype)


def flash(meta, queries_t, kv_all, steps):
    rows = queries_t.shape[1]
    group = HEADS // KV_HEADS
    width = group * HEAD_DIM

    def key_map(g, t, meta):
        return (jnp.minimum(meta[5] + t, meta[4]), g)

    def value_map(g, t, meta):
        return (jnp.minimum(meta[5] + t, meta[4]), KV_HEADS + g)

    spec = pltpu.PrefetchScalarGridSpec(
        num_scalar_prefetch=1,
        grid=(KV_HEADS, steps),
        in_specs=[
            pl.BlockSpec((width, rows), lambda g, t, meta: (g, 0)),
            pl.BlockSpec((BLOCK, HEAD_DIM), key_map),
            pl.BlockSpec((BLOCK, HEAD_DIM), value_map),
        ],
        out_specs=pl.BlockSpec((rows, width), lambda g, t, meta: (0, g)),
        scratch_shapes=[
            pltpu.VMEM((BLOCK, rows), jnp.float32),
            pltpu.VMEM((group, 1, rows), jnp.float32),
            pltpu.VMEM((group, 1, rows), jnp.float32),
            pltpu.VMEM((group, HEAD_DIM, rows), jnp.float32),
        ],
    )
    return pl.pallas_call(
        flash_body,
        grid_spec=spec,
        out_shape=jax.ShapeDtypeStruct((rows, HEADS * HEAD_DIM), jnp.bfloat16),
        compiler_params=pltpu.CompilerParams(dimension_semantics=("arbitrary", "arbitrary")),
    )(meta, queries_t, kv_all, kv_all)


def norm_rows(values, gain):
    wide = values.astype(jnp.float32)
    scale = lax.rsqrt(jnp.mean(wide * wide, axis=1, keepdims=True) + 1e-06)
    return (wide * scale * gain[None, :]).astype(jnp.bfloat16)


def segment_of(index, ends):
    return jnp.sum((ends[None, :] <= index[:, None]).astype(jnp.int32), axis=1)


def rotate(block, pos, heads):
    half = HEAD_DIM // 2
    freqs = 1000000.0 ** (-2.0 * jnp.arange(half, dtype=jnp.float32) / HEAD_DIM)
    angle = pos.astype(jnp.float32)[:, None, None] * freqs[None, None, :]
    wide = block.astype(jnp.float32).reshape(block.shape[0], heads, HEAD_DIM)
    first, second = (wide[..., :half], wide[..., half:])
    turned = jnp.concatenate(
        [
            first * jnp.cos(angle) - second * jnp.sin(angle),
            second * jnp.cos(angle) + first * jnp.sin(angle),
        ],
        axis=2,
    )
    return turned.reshape(block.shape[0], heads * HEAD_DIM).astype(jnp.bfloat16)


def project_joined(normed, weight, bias):
    rows, width = normed.shape[0], weight.shape[1]
    n_x = lax.axis_size("x")
    n_y = lax.axis_size("y")
    here = lax.axis_index("x")
    shifted = [normed]
    for step in range(1, n_x):
        pairs = [(s, (s + step) % n_x) for s in range(n_x)]
        shifted.append(lax.ppermute(normed, "x", pairs))
    pieces = lax.all_gather(weight, ("z", "c", "y"), axis=0, tiled=False)
    pieces = pieces.reshape(-1, n_y, weight.shape[0], width)
    bias_block = bias.reshape(n_y, n_x, width)
    bias_block = lax.dynamic_index_in_dim(bias_block, here, 1, keepdims=False)
    outs = []
    for piece in shifted:
        summed = jnp.einsum(
            "tie,iyec->tyc",
            piece.reshape(rows, pieces.shape[0], weight.shape[0]),
            pieces,
            preferred_element_type=jnp.float32,
        )
        outs.append((summed + bias_block[None]).astype(jnp.bfloat16))

    def exchange(take):
        full = jnp.zeros((rows, n_x) + take(outs[0]).shape[1:], outs[0].dtype)
        full = lax.dynamic_update_slice_in_dim(full, take(outs[0])[:, None], here, 1)
        for step in range(1, n_x):
            pairs = [(s, (s + step) % n_x) for s in range(n_x)]
            got = lax.ppermute(take(outs[(n_x - step) % n_x]), "x", pairs)
            full = lax.dynamic_update_slice_in_dim(full, got[:, None], (here - step) % n_x, 1)
        return full

    tail = exchange(lambda out: out[:, n_y - 1]).reshape(rows, -1)
    head = exchange(lambda out: out[:, : n_y - 1])
    head = jnp.transpose(head, (0, 2, 1, 3))
    return head.reshape(rows, -1), tail


def on_device(hidden_in, lengths, attn_norm, qkv_weight, qkv_bias):
    rows = hidden_in.shape[0]
    gy_index = lax.axis_index("y") * lax.axis_size("x") + lax.axis_index("x")
    first = gy_index * rows
    row_lengths = lengths[0]
    qdim = HEADS * HEAD_DIM
    kdim = KV_HEADS * HEAD_DIM
    group = HEADS // KV_HEADS
    normed = norm_rows(hidden_in, attn_norm)
    head, tail = project_joined(normed, qkv_weight, qkv_bias)
    split = qdim - head.shape[1]
    ends = jnp.cumsum(row_lengths)
    tokens_here = first + jnp.arange(rows, dtype=jnp.int32)
    before = ends[None, :] <= tokens_here[:, None]
    seg_here = jnp.sum(before.astype(jnp.int32), axis=1)
    begin = jnp.sum(jnp.where(before, row_lengths[None, :], 0), axis=1)
    pos = tokens_here - begin
    keys = rotate(tail[:, split : split + kdim], pos, KV_HEADS)
    kv_rows = jnp.concatenate([keys, tail[:, split + kdim :]], axis=1)
    queries = rotate(jnp.concatenate([head, tail[:, :split]], axis=1), pos, HEADS)
    piece = lax.all_gather(kv_rows, ("y", "x"), axis=0, tiled=True)
    lead = jnp.max(jnp.where(ends <= first, ends, 0))
    meta = jnp.concatenate(
        [ends, jnp.stack([gy_index, lead // BLOCK, 0, 0]).astype(jnp.int32)]
    ).astype(jnp.int32)
    steps = min(piece.shape[0] // BLOCK, 9)
    attn = flash(meta, jnp.transpose(queries), piece, steps)
    return (attn, kv_rows)


def solution(mesh):
    n_z = len({d.coords[2] for d in mesh.devices.flat})
    grid = mesh.devices.reshape(n_z, -1, *mesh.devices.shape[1:])
    n_y = len({d.coords[1] for d in mesh.devices.flat})
    grid = grid.reshape(grid.shape[0], grid.shape[1], n_y, -1)
    split = jax.sharding.Mesh(grid, ("z", "c", "y", "x"))
    tokens = P(("z", "c", "y", "x"), None)
    placed = (tokens, P(("z", "c"), None), P(), P(("z", "c"), ("y", "x")), P())
    return jax.shard_map(
        on_device,
        mesh=split,
        in_specs=placed,
        out_specs=(tokens, tokens),
        check_vma=False,
    )
```

```python
import math

import jax
import jax.numpy as jnp
from jax import lax
from jax.sharding import PartitionSpec as P
from jax.experimental import pallas as pl
from jax.experimental.pallas import tpu as pltpu

HEADS = 28
KV_HEADS = 4
HEAD_DIM = 128


BLOCK = 256


LANES = 128


def flash_body(meta, q_ref, k_ref, v_ref, o_ref, bias_ref, m_ref, l_ref, acc_ref):
    step = pl.program_id(0)
    last = pl.num_programs(0) - 1
    first = meta[4] * BLOCK
    block = jnp.minimum(meta[5] + step, meta[4])
    group = HEADS // KV_HEADS

    @pl.when(step == 0)
    def _():
        m_ref[...] = jnp.full(m_ref.shape, -1e30, jnp.float32)
        l_ref[...] = jnp.zeros(l_ref.shape, jnp.float32)
        acc_ref[...] = jnp.zeros(acc_ref.shape, jnp.float32)

    @pl.when(meta[5] + step <= meta[4])
    def _():
        krow = block * BLOCK + lax.broadcasted_iota(jnp.int32, (BLOCK, 1), 0)
        qcol = first + lax.broadcasted_iota(jnp.int32, (1, BLOCK), 1)
        qstart = jnp.zeros((1, BLOCK), jnp.int32)
        for s in range(4):
            end = meta[s]
            qstart = jnp.where(end <= qcol, end, qstart)
        allowed = (krow >= qstart) & (krow <= qcol)
        bias_ref[...] = jnp.where(allowed, 0.0, -1e30).astype(jnp.float32)
        scale = 1.0 / HEAD_DIM**0.5
        for g in range(KV_HEADS):
            dims = slice(g * HEAD_DIM, (g + 1) * HEAD_DIM)
            keys = k_ref[:, dims]
            values = jnp.transpose(v_ref[:, dims].astype(jnp.float32)).astype(jnp.bfloat16)
            for hh in range(group):
                h = g * group + hh
                heads = slice(h * HEAD_DIM, (h + 1) * HEAD_DIM)
                for c in range(BLOCK // LANES):
                    cols = slice(c * LANES, (c + 1) * LANES)
                    q = q_ref[heads, cols]
                    scores = (
                        jnp.dot(keys, q, preferred_element_type=jnp.float32) * scale
                        + bias_ref[:, cols]
                    )
                    m_prev = m_ref[h, :, cols]
                    m_new = jnp.maximum(m_prev, jnp.max(scores, axis=0, keepdims=True))
                    shrink = jnp.exp(m_prev - m_new)
                    weights = jnp.exp(scores - m_new)
                    l_ref[h, :, cols] = l_ref[h, :, cols] * shrink + jnp.sum(
                        weights, axis=0, keepdims=True
                    )
                    acc_ref[h, :, cols] = acc_ref[h, :, cols] * shrink + jnp.dot(
                        values, weights.astype(jnp.bfloat16), preferred_element_type=jnp.float32
                    )
                    m_ref[h, :, cols] = m_new

    @pl.when(step == last)
    def _():
        for h in range(HEADS):
            o_ref[:, h * HEAD_DIM : (h + 1) * HEAD_DIM] = jnp.transpose(
                acc_ref[h] / l_ref[h]
            ).astype(o_ref.dtype)


def flash(meta, queries_t, kv_all, steps):
    rows = queries_t.shape[1]
    width = HEADS * HEAD_DIM
    kdim = KV_HEADS * HEAD_DIM

    def key_map(t, meta):
        return (jnp.minimum(meta[5] + t, meta[4]), 0)

    def value_map(t, meta):
        return (jnp.minimum(meta[5] + t, meta[4]), 1)

    spec = pltpu.PrefetchScalarGridSpec(
        num_scalar_prefetch=1,
        grid=(steps,),
        in_specs=[
            pl.BlockSpec((width, rows), lambda t, meta: (0, 0)),
            pl.BlockSpec((BLOCK, kdim), key_map),
            pl.BlockSpec((BLOCK, kdim), value_map),
        ],
        out_specs=pl.BlockSpec((rows, width), lambda t, meta: (0, 0)),
        scratch_shapes=[
            pltpu.VMEM((BLOCK, rows), jnp.float32),
            pltpu.VMEM((HEADS, 1, rows), jnp.float32),
            pltpu.VMEM((HEADS, 1, rows), jnp.float32),
            pltpu.VMEM((HEADS, HEAD_DIM, rows), jnp.float32),
        ],
    )
    return pl.pallas_call(
        flash_body,
        grid_spec=spec,
        out_shape=jax.ShapeDtypeStruct((rows, width), jnp.bfloat16),
        compiler_params=pltpu.CompilerParams(dimension_semantics=("arbitrary",)),
    )(meta, queries_t, kv_all, kv_all)


def norm_rows(values, gain):
    wide = values.astype(jnp.float32)
    scale = lax.rsqrt(jnp.mean(wide * wide, axis=1, keepdims=True) + 1e-06)
    return (wide * scale * gain[None, :]).astype(jnp.bfloat16)


def segment_of(index, ends):
    return jnp.sum((ends[None, :] <= index[:, None]).astype(jnp.int32), axis=1)


def rotate(block, pos, heads):
    half = HEAD_DIM // 2
    freqs = 1000000.0 ** (-2.0 * jnp.arange(half, dtype=jnp.float32) / HEAD_DIM)
    angle = pos.astype(jnp.float32)[:, None, None] * freqs[None, None, :]
    wide = block.astype(jnp.float32).reshape(block.shape[0], heads, HEAD_DIM)
    first, second = (wide[..., :half], wide[..., half:])
    turned = jnp.concatenate(
        [
            first * jnp.cos(angle) - second * jnp.sin(angle),
            second * jnp.cos(angle) + first * jnp.sin(angle),
        ],
        axis=2,
    )
    return turned.reshape(block.shape[0], heads * HEAD_DIM).astype(jnp.bfloat16)


def project_joined(normed, weight, bias):
    rows, width = normed.shape[0], weight.shape[1]
    n_x = lax.axis_size("x")
    n_y = lax.axis_size("y")
    here = lax.axis_index("x")
    shifted = [normed]
    for step in range(1, n_x):
        pairs = [(s, (s + step) % n_x) for s in range(n_x)]
        shifted.append(lax.ppermute(normed, "x", pairs))
    pieces = lax.all_gather(weight, ("z", "c", "y"), axis=0, tiled=False)
    pieces = pieces.reshape(-1, n_y, weight.shape[0], width)
    bias_block = bias.reshape(n_y, n_x, width)
    bias_block = lax.dynamic_index_in_dim(bias_block, here, 1, keepdims=False)
    outs = []
    for piece in shifted:
        summed = jnp.einsum(
            "tie,iyec->tyc",
            piece.reshape(rows, pieces.shape[0], weight.shape[0]),
            pieces,
            preferred_element_type=jnp.float32,
        )
        outs.append((summed + bias_block[None]).astype(jnp.bfloat16))

    def exchange(take):
        full = jnp.zeros((rows, n_x) + take(outs[0]).shape[1:], outs[0].dtype)
        full = lax.dynamic_update_slice_in_dim(full, take(outs[0])[:, None], here, 1)
        for step in range(1, n_x):
            pairs = [(s, (s + step) % n_x) for s in range(n_x)]
            got = lax.ppermute(take(outs[(n_x - step) % n_x]), "x", pairs)
            full = lax.dynamic_update_slice_in_dim(full, got[:, None], (here - step) % n_x, 1)
        return full

    tail = exchange(lambda out: out[:, n_y - 1]).reshape(rows, -1)
    head = exchange(lambda out: out[:, : n_y - 1])
    head = jnp.transpose(head, (0, 2, 1, 3))
    return head.reshape(rows, -1), tail


def on_device(hidden_in, lengths, attn_norm, qkv_weight, qkv_bias):
    rows = hidden_in.shape[0]
    gy_index = lax.axis_index("y") * lax.axis_size("x") + lax.axis_index("x")
    first = gy_index * rows
    row_lengths = lengths[0]
    qdim = HEADS * HEAD_DIM
    kdim = KV_HEADS * HEAD_DIM
    group = HEADS // KV_HEADS
    normed = norm_rows(hidden_in, attn_norm)
    head, tail = project_joined(normed, qkv_weight, qkv_bias)
    split = qdim - head.shape[1]
    ends = jnp.cumsum(row_lengths)
    tokens_here = first + jnp.arange(rows, dtype=jnp.int32)
    before = ends[None, :] <= tokens_here[:, None]
    seg_here = jnp.sum(before.astype(jnp.int32), axis=1)
    begin = jnp.sum(jnp.where(before, row_lengths[None, :], 0), axis=1)
    pos = tokens_here - begin
    keys = rotate(tail[:, split : split + kdim], pos, KV_HEADS)
    kv_rows = jnp.concatenate([keys, tail[:, split + kdim :]], axis=1)
    queries = rotate(jnp.concatenate([head, tail[:, :split]], axis=1), pos, HEADS)
    piece = lax.all_gather(kv_rows, ("y", "x"), axis=0, tiled=True)
    lead = jnp.max(jnp.where(ends <= first, ends, 0))
    meta = jnp.concatenate(
        [ends, jnp.stack([gy_index, lead // BLOCK, 0, 0]).astype(jnp.int32)]
    ).astype(jnp.int32)
    steps = min(piece.shape[0] // BLOCK, 9)
    attn = flash(meta, jnp.transpose(queries), piece, steps)
    return (attn, kv_rows)


def solution(mesh):
    n_z = len({d.coords[2] for d in mesh.devices.flat})
    grid = mesh.devices.reshape(n_z, -1, *mesh.devices.shape[1:])
    n_y = len({d.coords[1] for d in mesh.devices.flat})
    grid = grid.reshape(grid.shape[0], grid.shape[1], n_y, -1)
    split = jax.sharding.Mesh(grid, ("z", "c", "y", "x"))
    tokens = P(("z", "c", "y", "x"), None)
    placed = (tokens, P(("z", "c"), None), P(), P(("z", "c"), ("y", "x")), P())
    return jax.shard_map(
        on_device,
        mesh=split,
        in_specs=placed,
        out_specs=(tokens, tokens),
        check_vma=False,
    )
```

```python
import math

import jax
import jax.numpy as jnp
from jax import lax
from jax.sharding import PartitionSpec as P
from jax.experimental import pallas as pl
from jax.experimental.pallas import tpu as pltpu

HEADS = 28
KV_HEADS = 4
HEAD_DIM = 128


BLOCK = 256


LANES = 128


def flash_body(meta, q_ref, k_ref, v_ref, o_ref, bias_ref, m_ref, l_ref, acc_ref):
    step = pl.program_id(0)
    last = pl.num_programs(0) - 1
    first = meta[4] * BLOCK
    block = jnp.minimum(meta[5] + step, meta[4])
    group = HEADS // KV_HEADS

    @pl.when(step == 0)
    def _():
        m_ref[...] = jnp.full(m_ref.shape, -1e30, jnp.float32)
        l_ref[...] = jnp.zeros(l_ref.shape, jnp.float32)
        acc_ref[...] = jnp.zeros(acc_ref.shape, jnp.float32)

    @pl.when(meta[5] + step <= meta[4])
    def _():
        krow = block * BLOCK + lax.broadcasted_iota(jnp.int32, (BLOCK, 1), 0)
        qcol = first + lax.broadcasted_iota(jnp.int32, (1, BLOCK), 1)
        qstart = jnp.zeros((1, BLOCK), jnp.int32)
        for s in range(4):
            end = meta[s]
            qstart = jnp.where(end <= qcol, end, qstart)
        allowed = (krow >= qstart) & (krow <= qcol)
        bias_ref[...] = jnp.where(allowed, 0.0, -1e30).astype(jnp.float32)
        scale = 1.0 / HEAD_DIM**0.5
        for g in range(KV_HEADS):
            dims = slice(g * HEAD_DIM, (g + 1) * HEAD_DIM)
            keys = k_ref[:, dims]
            values = jnp.transpose(v_ref[:, dims].astype(jnp.float32)).astype(jnp.bfloat16)
            for hh in range(group):
                h = g * group + hh
                heads = slice(h * HEAD_DIM, (h + 1) * HEAD_DIM)
                for c in range(BLOCK // LANES):
                    cols = slice(c * LANES, (c + 1) * LANES)
                    q = q_ref[heads, cols]
                    scores = (
                        jnp.dot(keys, q, preferred_element_type=jnp.float32) * scale
                        + bias_ref[:, cols]
                    )
                    m_prev = m_ref[h, :, cols]
                    m_new = jnp.maximum(m_prev, jnp.max(scores, axis=0, keepdims=True))
                    shrink = jnp.exp(m_prev - m_new)
                    weights = jnp.exp(scores - m_new)
                    l_ref[h, :, cols] = l_ref[h, :, cols] * shrink + jnp.sum(
                        weights, axis=0, keepdims=True
                    )
                    acc_ref[h, :, cols] = acc_ref[h, :, cols] * shrink + jnp.dot(
                        values, weights.astype(jnp.bfloat16), preferred_element_type=jnp.float32
                    )
                    m_ref[h, :, cols] = m_new

    @pl.when(step == last)
    def _():
        for h in range(HEADS):
            o_ref[:, h * HEAD_DIM : (h + 1) * HEAD_DIM] = jnp.transpose(
                acc_ref[h] / l_ref[h]
            ).astype(o_ref.dtype)


def flash(meta, queries_t, kv_all, steps):
    rows = queries_t.shape[1]
    width = HEADS * HEAD_DIM
    kdim = KV_HEADS * HEAD_DIM

    def key_map(t, meta):
        return (jnp.minimum(meta[5] + t, meta[4]), 0)

    def value_map(t, meta):
        return (jnp.minimum(meta[5] + t, meta[4]), 1)

    spec = pltpu.PrefetchScalarGridSpec(
        num_scalar_prefetch=1,
        grid=(steps,),
        in_specs=[
            pl.BlockSpec((width, rows), lambda t, meta: (0, 0)),
            pl.BlockSpec((BLOCK, kdim), key_map),
            pl.BlockSpec((BLOCK, kdim), value_map),
        ],
        out_specs=pl.BlockSpec((rows, width), lambda t, meta: (0, 0)),
        scratch_shapes=[
            pltpu.VMEM((BLOCK, rows), jnp.float32),
            pltpu.VMEM((HEADS, 1, rows), jnp.float32),
            pltpu.VMEM((HEADS, 1, rows), jnp.float32),
            pltpu.VMEM((HEADS, HEAD_DIM, rows), jnp.float32),
        ],
    )
    return pl.pallas_call(
        flash_body,
        grid_spec=spec,
        out_shape=jax.ShapeDtypeStruct((rows, width), jnp.bfloat16),
        compiler_params=pltpu.CompilerParams(dimension_semantics=("arbitrary",)),
    )(meta, queries_t, kv_all, kv_all)


def norm_rows(values, gain):
    wide = values.astype(jnp.float32)
    scale = lax.rsqrt(jnp.mean(wide * wide, axis=1, keepdims=True) + 1e-06)
    return (wide * scale * gain[None, :]).astype(jnp.bfloat16)


def segment_of(index, ends):
    return jnp.sum((ends[None, :] <= index[:, None]).astype(jnp.int32), axis=1)


def rotate(block, pos, heads):
    half = HEAD_DIM // 2
    freqs = 1000000.0 ** (-2.0 * jnp.arange(half, dtype=jnp.float32) / HEAD_DIM)
    angle = pos.astype(jnp.float32)[:, None, None] * freqs[None, None, :]
    wide = block.astype(jnp.float32).reshape(block.shape[0], heads, HEAD_DIM)
    first, second = (wide[..., :half], wide[..., half:])
    turned = jnp.concatenate(
        [
            first * jnp.cos(angle) - second * jnp.sin(angle),
            second * jnp.cos(angle) + first * jnp.sin(angle),
        ],
        axis=2,
    )
    return turned.reshape(block.shape[0], heads * HEAD_DIM).astype(jnp.bfloat16)


def project_joined(normed, weight, bias):
    rows, width = normed.shape[0], weight.shape[1]
    n_x = lax.axis_size("x")
    n_y = lax.axis_size("y")
    here = lax.axis_index("x")
    shifted = [normed]
    for step in range(1, n_x):
        pairs = [(s, (s + step) % n_x) for s in range(n_x)]
        shifted.append(lax.ppermute(normed, "x", pairs))
    pieces = lax.all_gather(weight, ("z", "c", "y"), axis=0, tiled=False)
    pieces = pieces.reshape(-1, n_y, weight.shape[0], width)
    bias_block = bias.reshape(n_y, n_x, width)
    bias_block = lax.dynamic_index_in_dim(bias_block, here, 1, keepdims=False)
    def project(part, part_bias):
        outs = []
        for piece in shifted:
            summed = jnp.einsum(
                "tie,iyec->tyc",
                piece.reshape(rows, pieces.shape[0], weight.shape[0]),
                part,
                preferred_element_type=jnp.float32,
            )
            outs.append((summed + part_bias[None]).astype(jnp.bfloat16))
        return outs

    def exchange(outs):
        full = jnp.zeros((rows, n_x) + outs[0].shape[1:], outs[0].dtype)
        full = lax.dynamic_update_slice_in_dim(full, outs[0][:, None], here, 1)
        for step in range(1, n_x):
            pairs = [(s, (s + step) % n_x) for s in range(n_x)]
            got = lax.ppermute(outs[(n_x - step) % n_x], "x", pairs)
            full = lax.dynamic_update_slice_in_dim(full, got[:, None], (here - step) % n_x, 1)
        return full

    tail = exchange(project(pieces[:, n_y - 1 :], bias_block[n_y - 1 :]))
    tail = tail.reshape(rows, -1)
    head = exchange(project(pieces[:, : n_y - 1], bias_block[: n_y - 1]))
    head = jnp.transpose(head, (0, 2, 1, 3))
    return head.reshape(rows, -1), tail


def on_device(hidden_in, lengths, attn_norm, qkv_weight, qkv_bias):
    rows = hidden_in.shape[0]
    gy_index = lax.axis_index("y") * lax.axis_size("x") + lax.axis_index("x")
    first = gy_index * rows
    row_lengths = lengths[0]
    qdim = HEADS * HEAD_DIM
    kdim = KV_HEADS * HEAD_DIM
    group = HEADS // KV_HEADS
    normed = norm_rows(hidden_in, attn_norm)
    head, tail = project_joined(normed, qkv_weight, qkv_bias)
    split = qdim - head.shape[1]
    ends = jnp.cumsum(row_lengths)
    tokens_here = first + jnp.arange(rows, dtype=jnp.int32)
    before = ends[None, :] <= tokens_here[:, None]
    seg_here = jnp.sum(before.astype(jnp.int32), axis=1)
    begin = jnp.sum(jnp.where(before, row_lengths[None, :], 0), axis=1)
    pos = tokens_here - begin
    keys = rotate(tail[:, split : split + kdim], pos, KV_HEADS)
    kv_rows = jnp.concatenate([keys, tail[:, split + kdim :]], axis=1)
    queries = rotate(jnp.concatenate([head, tail[:, :split]], axis=1), pos, HEADS)
    piece = lax.all_gather(kv_rows, ("y", "x"), axis=0, tiled=True)
    lead = jnp.max(jnp.where(ends <= first, ends, 0))
    meta = jnp.concatenate(
        [ends, jnp.stack([gy_index, lead // BLOCK, 0, 0]).astype(jnp.int32)]
    ).astype(jnp.int32)
    steps = min(piece.shape[0] // BLOCK, 9)
    attn = flash(meta, jnp.transpose(queries), piece, steps)
    return (attn, kv_rows)


def solution(mesh):
    n_z = len({d.coords[2] for d in mesh.devices.flat})
    grid = mesh.devices.reshape(n_z, -1, *mesh.devices.shape[1:])
    n_y = len({d.coords[1] for d in mesh.devices.flat})
    grid = grid.reshape(grid.shape[0], grid.shape[1], n_y, -1)
    split = jax.sharding.Mesh(grid, ("z", "c", "y", "x"))
    tokens = P(("z", "c", "y", "x"), None)
    placed = (tokens, P(("z", "c"), None), P(), P(("z", "c"), ("y", "x")), P())
    return jax.shard_map(
        on_device,
        mesh=split,
        in_specs=placed,
        out_specs=(tokens, tokens),
        check_vma=False,
    )
```

```python
import math

import jax
import jax.numpy as jnp
from jax import lax
from jax.sharding import PartitionSpec as P
from jax.experimental import pallas as pl
from jax.experimental.pallas import tpu as pltpu

HEADS = 28
KV_HEADS = 4
HEAD_DIM = 128


BLOCK = 256


LANES = 128


def flash_body(meta, q_ref, k_ref, v_ref, o_ref, bias_ref, m_ref, l_ref, acc_ref):
    step = pl.program_id(0)
    last = pl.num_programs(0) - 1
    first = meta[4] * BLOCK
    block = jnp.minimum(meta[5] + step, meta[4])
    group = HEADS // KV_HEADS

    @pl.when(step == 0)
    def _():
        m_ref[...] = jnp.full(m_ref.shape, -1e30, jnp.float32)
        l_ref[...] = jnp.zeros(l_ref.shape, jnp.float32)
        acc_ref[...] = jnp.zeros(acc_ref.shape, jnp.float32)

    @pl.when(meta[5] + step <= meta[4])
    def _():
        krow = block * BLOCK + lax.broadcasted_iota(jnp.int32, (BLOCK, 1), 0)
        qcol = first + lax.broadcasted_iota(jnp.int32, (1, BLOCK), 1)
        qstart = jnp.zeros((1, BLOCK), jnp.int32)
        for s in range(4):
            end = meta[s]
            qstart = jnp.where(end <= qcol, end, qstart)
        allowed = (krow >= qstart) & (krow <= qcol)
        bias_ref[...] = jnp.where(allowed, 0.0, -1e30).astype(jnp.float32)
        scale = math.log2(math.e) / HEAD_DIM**0.5
        for g in range(KV_HEADS):
            dims = slice(g * HEAD_DIM, (g + 1) * HEAD_DIM)
            keys = k_ref[:, dims]
            values = jnp.transpose(v_ref[:, dims].astype(jnp.float32)).astype(jnp.bfloat16)
            for hh in range(group):
                h = g * group + hh
                heads = slice(h * HEAD_DIM, (h + 1) * HEAD_DIM)
                for c in range(BLOCK // LANES):
                    cols = slice(c * LANES, (c + 1) * LANES)
                    q = q_ref[heads, cols]
                    scores = (
                        jnp.dot(keys, q, preferred_element_type=jnp.float32) + bias_ref[:, cols]
                    )
                    m_prev = m_ref[h, :, cols]
                    m_new = jnp.maximum(m_prev, jnp.max(scores, axis=0, keepdims=True))
                    shrink = jnp.exp2((m_prev - m_new) * scale)
                    weights = jnp.exp2((scores - m_new) * scale)
                    l_ref[h, :, cols] = l_ref[h, :, cols] * shrink + jnp.sum(
                        weights, axis=0, keepdims=True
                    )
                    acc_ref[h, :, cols] = acc_ref[h, :, cols] * shrink + jnp.dot(
                        values, weights.astype(jnp.bfloat16), preferred_element_type=jnp.float32
                    )
                    m_ref[h, :, cols] = m_new

    @pl.when(step == last)
    def _():
        for h in range(HEADS):
            o_ref[:, h * HEAD_DIM : (h + 1) * HEAD_DIM] = jnp.transpose(
                acc_ref[h] / l_ref[h]
            ).astype(o_ref.dtype)


def flash(meta, queries_t, kv_all, steps):
    rows = queries_t.shape[1]
    width = HEADS * HEAD_DIM
    kdim = KV_HEADS * HEAD_DIM

    def key_map(t, meta):
        return (jnp.minimum(meta[5] + t, meta[4]), 0)

    def value_map(t, meta):
        return (jnp.minimum(meta[5] + t, meta[4]), 1)

    spec = pltpu.PrefetchScalarGridSpec(
        num_scalar_prefetch=1,
        grid=(steps,),
        in_specs=[
            pl.BlockSpec((width, rows), lambda t, meta: (0, 0)),
            pl.BlockSpec((BLOCK, kdim), key_map),
            pl.BlockSpec((BLOCK, kdim), value_map),
        ],
        out_specs=pl.BlockSpec((rows, width), lambda t, meta: (0, 0)),
        scratch_shapes=[
            pltpu.VMEM((BLOCK, rows), jnp.float32),
            pltpu.VMEM((HEADS, 1, rows), jnp.float32),
            pltpu.VMEM((HEADS, 1, rows), jnp.float32),
            pltpu.VMEM((HEADS, HEAD_DIM, rows), jnp.float32),
        ],
    )
    return pl.pallas_call(
        flash_body,
        grid_spec=spec,
        out_shape=jax.ShapeDtypeStruct((rows, width), jnp.bfloat16),
        compiler_params=pltpu.CompilerParams(dimension_semantics=("arbitrary",)),
    )(meta, queries_t, kv_all, kv_all)


def norm_rows(values, gain):
    wide = values.astype(jnp.float32)
    scale = lax.rsqrt(jnp.mean(wide * wide, axis=1, keepdims=True) + 1e-06)
    return (wide * scale * gain[None, :]).astype(jnp.bfloat16)


def segment_of(index, ends):
    return jnp.sum((ends[None, :] <= index[:, None]).astype(jnp.int32), axis=1)


def rotate(block, pos, heads):
    half = HEAD_DIM // 2
    freqs = 1000000.0 ** (-2.0 * jnp.arange(half, dtype=jnp.float32) / HEAD_DIM)
    angle = pos.astype(jnp.float32)[:, None, None] * freqs[None, None, :]
    wide = block.astype(jnp.float32).reshape(block.shape[0], heads, HEAD_DIM)
    first, second = (wide[..., :half], wide[..., half:])
    turned = jnp.concatenate(
        [
            first * jnp.cos(angle) - second * jnp.sin(angle),
            second * jnp.cos(angle) + first * jnp.sin(angle),
        ],
        axis=2,
    )
    return turned.reshape(block.shape[0], heads * HEAD_DIM).astype(jnp.bfloat16)


def project_joined(normed, weight, bias):
    rows, width = normed.shape[0], weight.shape[1]
    n_x = lax.axis_size("x")
    n_y = lax.axis_size("y")
    here = lax.axis_index("x")
    shifted = [normed]
    for step in range(1, n_x):
        pairs = [(s, (s + step) % n_x) for s in range(n_x)]
        shifted.append(lax.ppermute(normed, "x", pairs))
    pieces = lax.all_gather(weight, ("z", "c", "y"), axis=0, tiled=False)
    pieces = pieces.reshape(-1, n_y, weight.shape[0], width)
    bias_block = bias.reshape(n_y, n_x, width)
    bias_block = lax.dynamic_index_in_dim(bias_block, here, 1, keepdims=False)
    def project(part, part_bias):
        outs = []
        for piece in shifted:
            summed = jnp.einsum(
                "tie,iyec->tyc",
                piece.reshape(rows, pieces.shape[0], weight.shape[0]),
                part,
                preferred_element_type=jnp.float32,
            )
            outs.append((summed + part_bias[None]).astype(jnp.bfloat16))
        return outs

    def exchange(outs):
        full = jnp.zeros((rows, n_x) + outs[0].shape[1:], outs[0].dtype)
        full = lax.dynamic_update_slice_in_dim(full, outs[0][:, None], here, 1)
        for step in range(1, n_x):
            pairs = [(s, (s + step) % n_x) for s in range(n_x)]
            got = lax.ppermute(outs[(n_x - step) % n_x], "x", pairs)
            full = lax.dynamic_update_slice_in_dim(full, got[:, None], (here - step) % n_x, 1)
        return full

    tail = exchange(project(pieces[:, n_y - 1 :], bias_block[n_y - 1 :]))
    tail = tail.reshape(rows, -1)
    head = exchange(project(pieces[:, : n_y - 1], bias_block[: n_y - 1]))
    head = jnp.transpose(head, (0, 2, 1, 3))
    return head.reshape(rows, -1), tail


def on_device(hidden_in, lengths, attn_norm, qkv_weight, qkv_bias):
    rows = hidden_in.shape[0]
    gy_index = lax.axis_index("y") * lax.axis_size("x") + lax.axis_index("x")
    first = gy_index * rows
    row_lengths = lengths[0]
    qdim = HEADS * HEAD_DIM
    kdim = KV_HEADS * HEAD_DIM
    group = HEADS // KV_HEADS
    normed = norm_rows(hidden_in, attn_norm)
    head, tail = project_joined(normed, qkv_weight, qkv_bias)
    split = qdim - head.shape[1]
    ends = jnp.cumsum(row_lengths)
    tokens_here = first + jnp.arange(rows, dtype=jnp.int32)
    before = ends[None, :] <= tokens_here[:, None]
    seg_here = jnp.sum(before.astype(jnp.int32), axis=1)
    begin = jnp.sum(jnp.where(before, row_lengths[None, :], 0), axis=1)
    pos = tokens_here - begin
    keys = rotate(tail[:, split : split + kdim], pos, KV_HEADS)
    kv_rows = jnp.concatenate([keys, tail[:, split + kdim :]], axis=1)
    queries = rotate(jnp.concatenate([head, tail[:, :split]], axis=1), pos, HEADS)
    piece = lax.all_gather(kv_rows, ("y", "x"), axis=0, tiled=True)
    lead = jnp.max(jnp.where(ends <= first, ends, 0))
    meta = jnp.concatenate(
        [ends, jnp.stack([gy_index, lead // BLOCK, 0, 0]).astype(jnp.int32)]
    ).astype(jnp.int32)
    steps = min(piece.shape[0] // BLOCK, 9)
    attn = flash(meta, jnp.transpose(queries), piece, steps)
    return (attn, kv_rows)


def solution(mesh):
    n_z = len({d.coords[2] for d in mesh.devices.flat})
    grid = mesh.devices.reshape(n_z, -1, *mesh.devices.shape[1:])
    n_y = len({d.coords[1] for d in mesh.devices.flat})
    grid = grid.reshape(grid.shape[0], grid.shape[1], n_y, -1)
    split = jax.sharding.Mesh(grid, ("z", "c", "y", "x"))
    tokens = P(("z", "c", "y", "x"), None)
    placed = (tokens, P(("z", "c"), None), P(), P(("z", "c"), ("y", "x")), P())
    return jax.shard_map(
        on_device,
        mesh=split,
        in_specs=placed,
        out_specs=(tokens, tokens),
        check_vma=False,
    )
```

```python
import math

import jax
import jax.numpy as jnp
from jax import lax
from jax.sharding import PartitionSpec as P
from jax.experimental import pallas as pl
from jax.experimental.pallas import tpu as pltpu

HEADS = 28
KV_HEADS = 4
HEAD_DIM = 128


BLOCK = 256


LANES = 128


def flash_body(meta, q_ref, k_ref, v_ref, o_ref, bias_ref, m_ref, l_ref, acc_ref):
    step = pl.program_id(0)
    last = pl.num_programs(0) - 1
    first = meta[4] * BLOCK
    block = jnp.minimum(meta[5] + step, meta[4])
    group = HEADS // KV_HEADS

    @pl.when(step == 0)
    def _():
        m_ref[...] = jnp.full(m_ref.shape, -1e30, jnp.float32)
        l_ref[...] = jnp.zeros(l_ref.shape, jnp.float32)
        acc_ref[...] = jnp.zeros(acc_ref.shape, jnp.float32)

    @pl.when(meta[5] + step <= meta[4])
    def _():
        krow = block * BLOCK + lax.broadcasted_iota(jnp.int32, (BLOCK, 1), 0)
        qcol = first + lax.broadcasted_iota(jnp.int32, (1, BLOCK), 1)
        qstart = jnp.zeros((1, BLOCK), jnp.int32)
        for s in range(4):
            end = meta[s]
            qstart = jnp.where(end <= qcol, end, qstart)
        allowed = (krow >= qstart) & (krow <= qcol)
        bias_ref[...] = jnp.where(allowed, 0.0, -1e30).astype(jnp.float32)
        scale = math.log2(math.e) / HEAD_DIM**0.5
        for g in range(KV_HEADS):
            dims = slice(g * HEAD_DIM, (g + 1) * HEAD_DIM)
            keys = k_ref[:, dims]
            values = jnp.transpose(v_ref[:, dims])
            for hh in range(group):
                h = g * group + hh
                heads = slice(h * HEAD_DIM, (h + 1) * HEAD_DIM)
                for c in range(BLOCK // LANES):
                    cols = slice(c * LANES, (c + 1) * LANES)
                    q = q_ref[heads, cols]
                    scores = (
                        jnp.dot(keys, q, preferred_element_type=jnp.float32) + bias_ref[:, cols]
                    )
                    m_prev = m_ref[h, :, cols]
                    m_new = jnp.maximum(m_prev, jnp.max(scores, axis=0, keepdims=True))
                    shrink = jnp.exp2((m_prev - m_new) * scale)
                    weights = jnp.exp2((scores - m_new) * scale)
                    l_ref[h, :, cols] = l_ref[h, :, cols] * shrink + jnp.sum(
                        weights, axis=0, keepdims=True
                    )
                    acc_ref[h, :, cols] = acc_ref[h, :, cols] * shrink + jnp.dot(
                        values, weights.astype(jnp.bfloat16), preferred_element_type=jnp.float32
                    )
                    m_ref[h, :, cols] = m_new

    @pl.when(step == last)
    def _():
        for h in range(HEADS):
            o_ref[:, h * HEAD_DIM : (h + 1) * HEAD_DIM] = jnp.transpose(
                acc_ref[h] / l_ref[h]
            ).astype(o_ref.dtype)


def flash(meta, queries_t, kv_all, steps):
    rows = queries_t.shape[1]
    width = HEADS * HEAD_DIM
    kdim = KV_HEADS * HEAD_DIM

    def key_map(t, meta):
        return (jnp.minimum(meta[5] + t, meta[4]), 0)

    def value_map(t, meta):
        return (jnp.minimum(meta[5] + t, meta[4]), 1)

    spec = pltpu.PrefetchScalarGridSpec(
        num_scalar_prefetch=1,
        grid=(steps,),
        in_specs=[
            pl.BlockSpec((width, rows), lambda t, meta: (0, 0)),
            pl.BlockSpec((BLOCK, kdim), key_map),
            pl.BlockSpec((BLOCK, kdim), value_map),
        ],
        out_specs=pl.BlockSpec((rows, width), lambda t, meta: (0, 0)),
        scratch_shapes=[
            pltpu.VMEM((BLOCK, rows), jnp.float32),
            pltpu.VMEM((HEADS, 1, rows), jnp.float32),
            pltpu.VMEM((HEADS, 1, rows), jnp.float32),
            pltpu.VMEM((HEADS, HEAD_DIM, rows), jnp.float32),
        ],
    )
    return pl.pallas_call(
        flash_body,
        grid_spec=spec,
        out_shape=jax.ShapeDtypeStruct((rows, width), jnp.bfloat16),
        compiler_params=pltpu.CompilerParams(dimension_semantics=("arbitrary",)),
    )(meta, queries_t, kv_all, kv_all)


def norm_rows(values, gain):
    wide = values.astype(jnp.float32)
    scale = lax.rsqrt(jnp.mean(wide * wide, axis=1, keepdims=True) + 1e-06)
    return (wide * scale * gain[None, :]).astype(jnp.bfloat16)


def segment_of(index, ends):
    return jnp.sum((ends[None, :] <= index[:, None]).astype(jnp.int32), axis=1)


def rotate(block, pos, heads):
    half = HEAD_DIM // 2
    freqs = 1000000.0 ** (-2.0 * jnp.arange(half, dtype=jnp.float32) / HEAD_DIM)
    angle = pos.astype(jnp.float32)[:, None, None] * freqs[None, None, :]
    wide = block.astype(jnp.float32).reshape(block.shape[0], heads, HEAD_DIM)
    first, second = (wide[..., :half], wide[..., half:])
    turned = jnp.concatenate(
        [
            first * jnp.cos(angle) - second * jnp.sin(angle),
            second * jnp.cos(angle) + first * jnp.sin(angle),
        ],
        axis=2,
    )
    return turned.reshape(block.shape[0], heads * HEAD_DIM).astype(jnp.bfloat16)


def project_joined(normed, weight, bias):
    rows, width = normed.shape[0], weight.shape[1]
    n_x = lax.axis_size("x")
    n_y = lax.axis_size("y")
    here = lax.axis_index("x")
    shifted = [normed]
    for step in range(1, n_x):
        pairs = [(s, (s + step) % n_x) for s in range(n_x)]
        shifted.append(lax.ppermute(normed, "x", pairs))
    pieces = lax.all_gather(weight, ("z", "c", "y"), axis=0, tiled=False)
    pieces = pieces.reshape(-1, n_y, weight.shape[0], width)
    bias_block = bias.reshape(n_y, n_x, width)
    bias_block = lax.dynamic_index_in_dim(bias_block, here, 1, keepdims=False)
    def project(part, part_bias):
        outs = []
        for piece in shifted:
            summed = jnp.einsum(
                "tie,iyec->tyc",
                piece.reshape(rows, pieces.shape[0], weight.shape[0]),
                part,
                preferred_element_type=jnp.float32,
            )
            outs.append((summed + part_bias[None]).astype(jnp.bfloat16))
        return outs

    def exchange(outs):
        full = jnp.zeros((rows, n_x) + outs[0].shape[1:], outs[0].dtype)
        full = lax.dynamic_update_slice_in_dim(full, outs[0][:, None], here, 1)
        for step in range(1, n_x):
            pairs = [(s, (s + step) % n_x) for s in range(n_x)]
            got = lax.ppermute(outs[(n_x - step) % n_x], "x", pairs)
            full = lax.dynamic_update_slice_in_dim(full, got[:, None], (here - step) % n_x, 1)
        return full

    tail = exchange(project(pieces[:, n_y - 1 :], bias_block[n_y - 1 :]))
    tail = tail.reshape(rows, -1)
    head = exchange(project(pieces[:, : n_y - 1], bias_block[: n_y - 1]))
    head = jnp.transpose(head, (0, 2, 1, 3))
    return head.reshape(rows, -1), tail


def on_device(hidden_in, lengths, attn_norm, qkv_weight, qkv_bias):
    rows = hidden_in.shape[0]
    gy_index = lax.axis_index("y") * lax.axis_size("x") + lax.axis_index("x")
    first = gy_index * rows
    row_lengths = lengths[0]
    qdim = HEADS * HEAD_DIM
    kdim = KV_HEADS * HEAD_DIM
    group = HEADS // KV_HEADS
    normed = norm_rows(hidden_in, attn_norm)
    head, tail = project_joined(normed, qkv_weight, qkv_bias)
    split = qdim - head.shape[1]
    ends = jnp.cumsum(row_lengths)
    tokens_here = first + jnp.arange(rows, dtype=jnp.int32)
    before = ends[None, :] <= tokens_here[:, None]
    seg_here = jnp.sum(before.astype(jnp.int32), axis=1)
    begin = jnp.sum(jnp.where(before, row_lengths[None, :], 0), axis=1)
    pos = tokens_here - begin
    keys = rotate(tail[:, split : split + kdim], pos, KV_HEADS)
    kv_rows = jnp.concatenate([keys, tail[:, split + kdim :]], axis=1)
    queries = rotate(jnp.concatenate([head, tail[:, :split]], axis=1), pos, HEADS)
    piece = lax.all_gather(kv_rows, ("y", "x"), axis=0, tiled=True)
    lead = jnp.max(jnp.where(ends <= first, ends, 0))
    meta = jnp.concatenate(
        [ends, jnp.stack([gy_index, lead // BLOCK, 0, 0]).astype(jnp.int32)]
    ).astype(jnp.int32)
    steps = min(piece.shape[0] // BLOCK, 9)
    attn = flash(meta, jnp.transpose(queries), piece, steps)
    return (attn, kv_rows)


def solution(mesh):
    n_z = len({d.coords[2] for d in mesh.devices.flat})
    grid = mesh.devices.reshape(n_z, -1, *mesh.devices.shape[1:])
    n_y = len({d.coords[1] for d in mesh.devices.flat})
    grid = grid.reshape(grid.shape[0], grid.shape[1], n_y, -1)
    split = jax.sharding.Mesh(grid, ("z", "c", "y", "x"))
    tokens = P(("z", "c", "y", "x"), None)
    placed = (tokens, P(("z", "c"), None), P(), P(("z", "c"), ("y", "x")), P())
    return jax.shard_map(
        on_device,
        mesh=split,
        in_specs=placed,
        out_specs=(tokens, tokens),
        check_vma=False,
    )
```
